256 devices in a mesh: dp: 4 (over y), expert: 64 (over z, x, core).
Axes of the slice: x: 4, y: 4, z: 8, core: 2. Of those that a mesh axis runs over, the one named last changes fastest.
Arguments:
- tokens: bfloat16 [4096, 2048], P('expert'), may hold values from -6 to 6
- attn_gain: float32 [2048], replicated, may hold values from 0.5 to 1.5
- w_query: bfloat16 [2048, 2048], P('expert', 'dp'), may hold values from -0.125 to 0.125
- w_key: bfloat16 [2048, 2048], P('expert', 'dp'), may hold values from -0.125 to 0.125
- w_value: bfloat16 [2048, 2048], P('expert', 'dp'), may hold values from -0.125 to 0.125
- w_out: bfloat16 [2048, 2048], P('expert', 'dp'), may hold values from -0.125 to 0.125
- cache: bfloat16 [131072, 4096], P('expert', 'dp')
- page_table: int32 [64, 16], P('expert'), may hold values from 0 to 15, each once within a row
- cache_len: int32 [64, 4], P('expert'), may hold values from 1 to 512, 1024 in all within a row
- new_len: int32 [64, 4], P('expert'), may hold values from 1 to 32, 64 in all within a row
- kv_owner: int32 [4096, 1], P('expert'), may hold values from 0 to 63; in each aligned block of 64 rows (0 to 63, 64 to 127, ...) at most 2 rows name the same one
- moe_gain: float32 [2048], replicated, may hold values from 0.5 to 1.5
- w_gate: bfloat16 [64, 2048, 1024], P('expert', None, 'dp'), may hold values from -0.125 to 0.125
- w_up: bfloat16 [64, 2048, 1024], P('expert', None, 'dp'), may hold values from -0.125 to 0.125
- w_down: bfloat16 [64, 1024, 2048], P('expert', 'dp'), may hold values from -0.1875 to 0.1875
- expert_ids: int32 [4096, 8], P('expert'), may hold values from 0 to 63, all different within a row; in each aligned block of 64 rows (0 to 63, 64 to 127, ...) at most 16 rows name the same one
- gate_weights: float32 [4096, 8], P('expert'), may hold values from 0.05 to 0.5
Outputs:
- out: bfloat16 [4096, 2048], P('expert')
- new_rows: bfloat16 [8192, 4096], P('expert', 'dp')
The draws below stay inside these ranges and needn't reach their ends.
Inputs may be any that keep to these rules, and one draw needn't show every extreme that they name: `page_table`: each row of one index of the expert axis lists every local page once; request r reserves the pages in entries r * 4 to (r+1) * 4 - 1. `cache_len`: the lengths of one index sum to 4 * 4 * 128 // 2, and one of them equals 512. `new_len`: the new tokens of one index sum to 64 and stand request by request; one request has exactly 64 // 2. `kv_owner`: among the rows of one device no owner is named more than 2 times; some owner is named exactly 2 times. `expert_ids`: each row names distinct experts; among the rows of one device no expert is named more than 16 times, a bound that some block reaches.
All inputs are finite; a program needn't handle non-finite values.
Results may differ from the reference program's by a relative error of at most 0.012.
The reference program's roundings to bfloat16 on the way (of `normed`, `probs`, `heads_out`, `moe_in`, `active` and `parts`) count: a program that leaves them out, or rounds other values in their place, can miss the bound.
Values may be sent and summed in bfloat16 or wider, within the bound.
No kernel may reach another device: no remote copies, remote signals or barrier semaphores. Data moves between devices by JAX's collectives and lax.ppermute only.
A program may use at most 64 MiB of HBM per device.

```python
import math
import jax
import jax.numpy as jnp
import numpy as np
from jax import lax

D = 2048
HEADS = 16
HD = 128
FF = 1024
TOP = 8
TOK_DEV = 64
REQ_DEV = 4
PAGE = 128
PAGES_REQ = 4
PAGES_DEV = 16
EXPERTS = 64
TOKENS = 4096
CAP = 16
KCAP = 2
POOL_DEV = 128
N_DP = 4
N_EXPERT = 64


def draw_cache(key, part):
    row_total = N_EXPERT * PAGES_DEV * PAGE
    feat_total = 2 * HEADS * HD
    base = jax.random.normal(key, (row_total, feat_total), jnp.float32)
    return base.astype(jnp.bfloat16)


def block_levels(rng, dims, shards, smallest, high):
    level = 1.0
    for dim, blocks in shards:
        heights = jax.random.uniform(jax.random.fold_in(jax.random.fold_in(rng, 6), dim), (blocks,), jnp.float32, smallest / len(shards), high / len(shards))
        level = level * jnp.repeat(jnp.exp(heights), dims[dim] // blocks).reshape((-1,) + (1,) * (len(dims) - 1 - dim))
    return level


def profile(number_of, total, most, slope):
    weights = [(1 << 20) // math.isqrt(standing ** slope) + 1 for standing in range(2, number_of + 1)]
    surplus, given = total - most - (number_of - 1), [1] * (number_of - 1)
    while surplus > 0:
        free = [i for i in range(number_of - 1) if given[i] < most]
        whole, left = sum([weights[i] for i in free]), surplus
        for i in free:
            more = min(most - given[i], max(1, left * weights[i] // whole), surplus)
            given[i] = given[i] + more
            surplus = surplus - more
    return np.array([most] + given)


def ragged_sizes(key, amount, total, bound, lean):
    if amount == 2:
        one = jax.random.randint(key, (), max(1, total - bound), min(bound, total - 1) + 1)
        return jnp.stack([one, total - one])
    tallies = jnp.asarray(profile(amount, total, bound, lean), jnp.int32)
    couples = (amount - 1) // 2
    source_of, receiver = tallies[1:1 + 2 * couples:2], tallies[2:2 + 2 * couples:2]
    margin = jnp.minimum(source_of - 1, bound - receiver)
    shifted = jax.random.randint(jax.random.fold_in(key, 1), (couples,), 0, 1 << 20) % (margin + 1)
    tallies = tallies.at[1:1 + 2 * couples:2].set(source_of - shifted).at[2:2 + 2 * couples:2].set(receiver + shifted)
    return tallies[jax.random.permutation(jax.random.fold_in(key, 2), amount)]


def assign_block(key, own, number, rows, count, top, reach, lean):
    sequence = jax.random.permutation(key, count)
    crowded, ordinary = load_shares(count, rows * top, reach, lean, True), load_shares(count, rows * top, reach, lean, False)
    places = jnp.arange(count)

    def named(sizes, offset_by):
        used = int((sizes > 0).sum())
        fixed = max(1, used // 4)
        shifted = fixed + (places - fixed + offset_by * (used - fixed)) % max(1, count - fixed)
        return jnp.zeros((count,), jnp.int32).at[sequence[jnp.where(places < fixed, places, shifted)]].set(jnp.asarray(sizes, jnp.int32))

    sizes = jnp.where(number % 4 == 0, named(crowded, number // 4), named(ordinary, number - number // 4 - 1))
    mixed = jax.random.permutation(jax.random.fold_in(own, 3), count)
    giver, taker = mixed[0:count // 2 * 2:2], mixed[1:count // 2 * 2:2]
    room = jnp.minimum(sizes[giver] - 1, reach - sizes[taker]) // 2
    room = jnp.where((giver == sequence[0]) | (taker == sequence[0]) | (sizes[taker] == 0), 0, jnp.maximum(room, 0))
    shifted = jax.random.randint(jax.random.fold_in(own, 4), (count // 2,), 0, 1 << 20) % (room + 1)
    sizes = sizes.at[giver].add(-shifted).at[taker].add(shifted)
    items = jnp.searchsorted(jnp.cumsum(sizes), jnp.arange(rows * top), side="right").astype(jnp.int32)
    grid = items.reshape(top, rows).T
    grid = grid[jax.random.permutation(jax.random.fold_in(own, 1), rows)]
    offset_by = jax.random.randint(jax.random.fold_in(own, 2), (rows, 1), 0, top)
    return jnp.take_along_axis(grid, (jnp.arange(top)[None, :] + offset_by) % top, axis=1)


def load_shares(amount, total, reach, skew, full):
    portions = [(1 << 20) // math.isqrt(standing ** skew) + 1 for standing in range(1, amount + 1)]
    largest = reach if full else min(reach, max(-(-total // amount), total * portions[0] // sum(portions)))
    least = 1 if total - largest >= amount - 1 else 0
    given, rest = [largest] + [least] * (amount - 1), total - largest - least * (amount - 1)
    while rest > 0:
        candidates = [i for i in range(1, amount) if given[i] < largest] or [i for i in range(1, amount) if given[i] < reach]
        mass, left = sum([portions[i] for i in candidates]), rest
        for i in candidates:
            addition = min(reach - given[i], max(1, left * portions[i] // mass), rest)
            given[i] = given[i] + addition
            rest = rest - addition
    return np.array(given)


def scatter_about(stream_key, dims, width, most, cuts=(), kind=jnp.bfloat16):
    level = block_levels(stream_key, dims, cuts, -0.22, 0.18) if cuts else 1.0
    entries = jax.random.normal(stream_key, dims, jnp.float32) * width * level
    return jnp.minimum(jnp.maximum(entries, -most), most).astype(kind)


def setup_inputs(seed: int = 0) -> dict:
    key_of = jax.random.split(jax.random.key(seed), 18)
    tokens = scatter_about(key_of[0], (TOKENS, D), 1.0, 6.0, ((0, 64),))
    attn_gain = jnp.clip(1.0 + 0.1 * jax.random.normal(key_of[1], (D,), jnp.float32), 0.5, 1.5)
    w_query = scatter_about(key_of[2], (D, HEADS * HD), D ** -0.5, 0.125, ((0, 64), (1, 4)))
    w_key = scatter_about(key_of[3], (D, HEADS * HD), D ** -0.5, 0.125, ((0, 64), (1, 4)))
    w_value = scatter_about(key_of[4], (D, HEADS * HD), D ** -0.5, 0.125, ((0, 64), (1, 4)))
    w_out = scatter_about(key_of[5], (D, HEADS * HD), (HEADS * HD) ** -0.5, 0.125, ((0, 64), (1, 4)))
    cache = draw_cache(jax.random.fold_in(key_of[17], 71), 0)
    page_table = jax.vmap(lambda own: jax.random.permutation(own, PAGES_DEV))(jax.random.split(key_of[7], N_EXPERT)).reshape((N_EXPERT, PAGES_DEV)).astype(jnp.int32)
    cache_len = jax.vmap(lambda own: ragged_sizes(own, REQ_DEV, REQ_DEV * PAGES_REQ * PAGE // 2, PAGES_REQ * PAGE, 2))(jax.random.split(key_of[8], N_EXPERT)).reshape((N_EXPERT, REQ_DEV)).astype(jnp.int32)
    new_len = jax.vmap(lambda own: ragged_sizes(own, REQ_DEV, TOK_DEV, TOK_DEV // 2, 2))(jax.random.split(key_of[9], N_EXPERT)).reshape((N_EXPERT, REQ_DEV)).astype(jnp.int32)
    kv_owner_keys = jax.random.split(jax.random.fold_in(key_of[10], 1), TOKENS // TOK_DEV)
    kv_owner_turns = jax.random.permutation(jax.random.fold_in(key_of[10], 3), TOKENS // TOK_DEV)
    kv_owner = jax.vmap(lambda own, number: assign_block(jax.random.fold_in(key_of[10], 2), own, number, TOK_DEV, N_EXPERT, 1, KCAP, 1))(kv_owner_keys, kv_owner_turns).reshape((TOKENS, 1))
    moe_gain = jnp.clip(1.0 + 0.1 * jax.random.normal(key_of[11], (D,), jnp.float32), 0.5, 1.5)
    w_gate = scatter_about(key_of[12], (EXPERTS, D, FF), D ** -0.5, 0.125, ((0, 64), (2, 4)))
    w_up = scatter_about(key_of[13], (EXPERTS, D, FF), D ** -0.5, 0.125, ((0, 64), (2, 4)))
    w_down = scatter_about(key_of[14], (EXPERTS, FF, D), FF ** -0.5, 0.1875, ((0, 64), (1, 4)))
    expert_ids_keys = jax.random.split(jax.random.fold_in(key_of[15], 1), TOKENS // TOK_DEV)
    expert_ids_turns = jax.random.permutation(jax.random.fold_in(key_of[15], 3), TOKENS // TOK_DEV)
    expert_ids = jax.vmap(lambda own, number: assign_block(jax.random.fold_in(key_of[15], 2), own, number, TOK_DEV, EXPERTS, TOP, CAP, 2))(expert_ids_keys, expert_ids_turns).reshape((TOKENS, TOP))
    gate_weights = jnp.clip(jnp.exp(math.log(0.5) - 2.3025851 * jax.random.uniform(key_of[16], (TOKENS, TOP), jnp.float32) ** block_levels(key_of[16], (TOKENS, TOP), ((0, 64),), -0.2, 0.2)), 0.05, 0.5)
    return {"tokens": tokens, "attn_gain": attn_gain, "w_query": w_query, "w_key": w_key, "w_value": w_value, "w_out": w_out, "cache": cache, "page_table": page_table, "cache_len": cache_len, "new_len": new_len, "kv_owner": kv_owner, "moe_gain": moe_gain, "w_gate": w_gate, "w_up": w_up, "w_down": w_down, "expert_ids": expert_ids, "gate_weights": gate_weights}


EPSILON = 1e-05

def norm_rows(row_data, gain_vec):
    mean_sq = lax.optimization_barrier(jnp.mean(row_data * row_data, axis=-1, keepdims=True))
    return (row_data * lax.rsqrt(mean_sq + EPSILON) * gain_vec).astype(jnp.bfloat16)

def route_rank(route_ids, block_rows, id_range):
    row_total = route_ids.shape[0]
    labels = jnp.arange(id_range, dtype=jnp.int32)
    counts = lax.optimization_barrier(jnp.sum((route_ids[:, :, None] == labels[None, None, :]).astype(jnp.int32), axis=1)).astype(jnp.int32)
    counts = counts.reshape(row_total // block_rows, block_rows, id_range)
    before = (jnp.cumsum(counts, axis=1).astype(jnp.int32) - counts).reshape(row_total, id_range)
    return jnp.take_along_axis(before, route_ids, axis=1).astype(jnp.int32)

def key_masks(table_row, cache_lens, new_lens, row_count, page_size):
    req_count = cache_lens.shape[0]
    pages_here = table_row.shape[0]
    per_request = pages_here // req_count
    slot_ids = jnp.arange(pages_here, dtype=jnp.int32)
    matches = (table_row[:, None] == slot_ids[None, :]).astype(jnp.int32)
    slot_of_page = lax.optimization_barrier(jnp.sum(matches * slot_ids[:, None], axis=0)).astype(jnp.int32)
    page_request = slot_of_page // per_request
    page_start = slot_of_page % per_request * page_size
    key_request = jnp.repeat(page_request, page_size)
    key_position = jnp.repeat(page_start, page_size) + jnp.tile(jnp.arange(page_size, dtype=jnp.int32), pages_here)
    request_ids = jnp.arange(req_count, dtype=jnp.int32)
    key_length = lax.optimization_barrier(jnp.sum((key_request[:, None] == request_ids[None, :]).astype(jnp.int32) * cache_lens[None, :], axis=1)).astype(jnp.int32)
    request_ends = jnp.cumsum(new_lens).astype(jnp.int32)
    tok_ids = jnp.arange(row_count, dtype=jnp.int32)
    tok_request = lax.optimization_barrier(jnp.sum((tok_ids[:, None] >= request_ends[None, :]).astype(jnp.int32), axis=1)).astype(jnp.int32)
    cached = (tok_request[:, None] == key_request[None, :]) & (key_position < key_length)[None, :]
    fresh_mask = tok_request[:, None] == tok_request[None, :]
    return jnp.concatenate([cached, fresh_mask], axis=1)

def attention_block(token_rows, cache_rows, table_row, cache_lens, new_lens, attn_gain, w_query, w_key, w_value, w_out, moe_gain):
    row_count = token_rows.shape[0]
    cache_count = cache_rows.shape[0]
    per_group = HEADS // N_DP
    resid_in = token_rows.astype(jnp.float32)
    normed = norm_rows(resid_in, attn_gain)
    queries = jnp.dot(normed, w_query, preferred_element_type=jnp.float32).astype(jnp.bfloat16)
    new_keys = jnp.dot(normed, w_key, preferred_element_type=jnp.float32).astype(jnp.bfloat16)
    new_values = jnp.dot(normed, w_value, preferred_element_type=jnp.float32).astype(jnp.bfloat16)
    split_cache = cache_rows.reshape(cache_count, N_DP, 2, per_group, HD)
    all_keys = jnp.concatenate([split_cache[:, :, 0].reshape(cache_count, HEADS, HD), new_keys.reshape(row_count, HEADS, HD)], axis=0).astype(jnp.float32)
    all_values = jnp.concatenate([split_cache[:, :, 1].reshape(cache_count, HEADS, HD), new_values.reshape(row_count, HEADS, HD)], axis=0).astype(jnp.float32)
    scores = jnp.einsum('thc,rhc->htr', queries.reshape(row_count, HEADS, HD).astype(jnp.float32), all_keys) * HD ** (-0.5)
    valid_mask = key_masks(table_row, cache_lens, new_lens, row_count, PAGE)
    scores = jnp.where(valid_mask[None, :, :], scores, -1e+30)
    highest = lax.optimization_barrier(jnp.max(scores, axis=-1, keepdims=True))
    weights = jnp.exp(scores - highest)
    probs = (weights / lax.optimization_barrier(jnp.sum(weights, axis=-1, keepdims=True))).astype(jnp.bfloat16)
    heads_out = jnp.einsum('htr,rhc->thc', probs.astype(jnp.float32), all_values).astype(jnp.bfloat16).reshape(row_count, HEADS * HD)
    attn_out = jnp.dot(heads_out, w_out.T, preferred_element_type=jnp.float32)
    residual = resid_in + attn_out
    moe_in = norm_rows(residual, moe_gain)
    kv_rows = jnp.stack([new_keys.reshape(row_count, N_DP, per_group * HD), new_values.reshape(row_count, N_DP, per_group * HD)], axis=2).reshape(row_count, 2 * HEADS * HD)
    return (residual, moe_in, kv_rows)

def reference(tokens, attn_gain, w_query, w_key, w_value, w_out, cache, page_table, cache_len, new_len, kv_owner, moe_gain, w_gate, w_up, w_down, expert_ids, gate_weights):

    def per_device(pieces):
        return attention_block(pieces[0], pieces[1], pieces[2], pieces[3], pieces[4], attn_gain, w_query, w_key, w_value, w_out, moe_gain)
    residual, moe_in, kv_rows = lax.map(per_device, (tokens.reshape(N_EXPERT, TOK_DEV, D), cache.reshape(N_EXPERT, -1, cache.shape[1]), page_table, cache_len, new_len))
    residual = residual.reshape(N_EXPERT * TOK_DEV, D)
    moe_flat = moe_in.reshape(N_EXPERT * TOK_DEV, D)
    kv_flat = kv_rows.reshape(N_EXPERT * TOK_DEV, kv_rows.shape[-1])
    token_ids = jnp.arange(N_EXPERT * TOK_DEV, dtype=jnp.int32)
    sources = token_ids // TOK_DEV
    kv_rank = route_rank(kv_owner, TOK_DEV, N_EXPERT)[:, 0]
    dest_rows = kv_owner[:, 0] * POOL_DEV + sources * KCAP + kv_rank
    new_rows = jnp.zeros((N_EXPERT * POOL_DEV, kv_flat.shape[1]), jnp.bfloat16).at[dest_rows].set(kv_flat)
    slot_rank = route_rank(expert_ids, TOK_DEV, EXPERTS)
    columns = sources[:, None] * CAP + slot_rank
    holders = jnp.broadcast_to(token_ids[:, None], expert_ids.shape)
    index_table = jnp.zeros((EXPERTS, N_EXPERT * CAP), jnp.int32).at[expert_ids, columns].set(holders)
    gate_table = jnp.zeros((EXPERTS, N_EXPERT * CAP), jnp.float32).at[expert_ids, columns].set(gate_weights)
    slice_width = FF // N_DP

    def one_expert(running, pieces):
        row_index, gate_col, gate_mat, up_mat, down_mat = pieces
        picked = moe_flat[row_index]
        gate_proj = jnp.dot(picked, gate_mat, preferred_element_type=jnp.float32)
        up_proj = jnp.dot(picked, up_mat, preferred_element_type=jnp.float32)
        active = (jax.nn.silu(gate_proj) * up_proj).astype(jnp.bfloat16)
        parts = jnp.einsum('rnf,nfd->nrd', active.reshape(-1, N_DP, slice_width).astype(jnp.float32), down_mat.reshape(N_DP, slice_width, D).astype(jnp.float32)).astype(jnp.bfloat16)
        contrib = lax.optimization_barrier(jnp.sum(parts.astype(jnp.float32), axis=0))
        return (running.at[row_index].add(gate_col[:, None] * contrib), None)
    moe_total, unused = lax.scan(one_expert, jnp.zeros((N_EXPERT * TOK_DEV, D), jnp.float32), (index_table, gate_table, w_gate, w_up, w_down))
    out = (residual + moe_total).astype(jnp.bfloat16)
    return (out, new_rows)
```

```python
import jax
import jax.numpy as jnp
from jax import lax
from jax.sharding import PartitionSpec as P

HD = 128
PAGE = 128


EPSILON = 1e-05


def norm_rows(row_data, gain_vec):
    mean_sq = jnp.mean(row_data * row_data, axis=-1, keepdims=True)
    return (row_data * lax.rsqrt(mean_sq + EPSILON) * gain_vec).astype(jnp.bfloat16)


def route_rank(route_ids, block_rows, id_range):
    row_total = route_ids.shape[0]
    labels = jnp.arange(id_range, dtype=jnp.int32)
    counts = jnp.sum((route_ids[:, :, None] == labels[None, None, :]).astype(jnp.int32), axis=1)
    counts = counts.reshape(row_total // block_rows, block_rows, id_range)
    before = (jnp.cumsum(counts, axis=1) - counts).reshape(row_total, id_range)
    return jnp.take_along_axis(before, route_ids, axis=1)


def key_masks(table_row, cache_lens, new_lens, row_count, page_size):
    req_count = cache_lens.shape[0]
    pages_here = table_row.shape[0]
    per_request = pages_here // req_count
    slot_ids = jnp.arange(pages_here, dtype=jnp.int32)
    matches = (table_row[:, None] == slot_ids[None, :]).astype(jnp.int32)
    slot_of_page = jnp.sum(matches * slot_ids[:, None], axis=0)
    page_request = slot_of_page // per_request
    page_start = slot_of_page % per_request * page_size
    key_request = jnp.repeat(page_request, page_size)
    key_position = jnp.repeat(page_start, page_size) + jnp.tile(
        jnp.arange(page_size, dtype=jnp.int32), pages_here
    )
    request_ids = jnp.arange(req_count, dtype=jnp.int32)
    key_length = jnp.sum(
        (key_request[:, None] == request_ids[None, :]).astype(jnp.int32) * cache_lens[None, :],
        axis=1,
    )
    request_ends = jnp.cumsum(new_lens)
    tok_ids = jnp.arange(row_count, dtype=jnp.int32)
    tok_request = jnp.sum((tok_ids[:, None] >= request_ends[None, :]).astype(jnp.int32), axis=1)
    cached = (tok_request[:, None] == key_request[None, :]) & (key_position < key_length)[None, :]
    fresh_mask = tok_request[:, None] == tok_request[None, :]
    return jnp.concatenate([cached, fresh_mask], axis=1)


def dp_sum(part):
    n_dp = lax.axis_size("dp")
    me = lax.axis_index("dp")
    held = [part] + [
        lax.ppermute(part, "dp", [(i, (i + s) % n_dp) for i in range(n_dp)])
        for s in range(1, n_dp)
    ]
    held = jnp.stack(held).astype(jnp.float32)
    order = (me - jnp.arange(n_dp, dtype=jnp.int32)) % n_dp
    ordered = held[order]
    total = ordered[0]
    for j in range(1, n_dp):
        total = total + ordered[j]
    return total


def one_hot_rows(slots, slot_count):
    hits = slots[None, :, :] == jnp.arange(slot_count, dtype=jnp.int32)[:, None, None]
    return jnp.any(hits, axis=2).astype(jnp.bfloat16)


def place_rows(pick, rows):
    return jnp.dot(pick, rows, preferred_element_type=jnp.float32).astype(jnp.bfloat16)


def expert_block(routed, w_gate, w_up, w_down):
    gate_proj = jnp.einsum("necd,edf->necf", routed, w_gate, preferred_element_type=jnp.float32)
    up_proj = jnp.einsum("necd,edf->necf", routed, w_up, preferred_element_type=jnp.float32)
    active = (jax.nn.silu(gate_proj) * up_proj).astype(jnp.bfloat16)
    return jnp.einsum("necf,efd->necd", active, w_down, preferred_element_type=jnp.float32).astype(
        jnp.bfloat16
    )


def local(
    tokens,
    attn_gain,
    w_query,
    w_key,
    w_value,
    w_out,
    cache,
    page_table,
    cache_len,
    new_len,
    kv_owner,
    moe_gain,
    w_gate,
    w_up,
    w_down,
    expert_ids,
    gate_weights,
):
    row_count, model_width = tokens.shape
    n_expert = lax.axis_size("expert")
    local_experts = w_gate.shape[0]
    experts_all = n_expert * local_experts
    top_count = expert_ids.shape[1]
    capacity = min(row_count, 2 * row_count * top_count // experts_all)
    kv_cap = max(2, 2 * row_count // n_expert)
    head_group = w_query.shape[1] // HD
    stacked = lax.all_gather(
        jnp.stack([w_query, w_key, w_value, w_out]), "expert", axis=1, tiled=True
    )
    full_query, full_key, full_value, full_out = (
        stacked[0],
        stacked[1],
        stacked[2],
        stacked[3],
    )
    resid_in = tokens.astype(jnp.float32)
    normed = norm_rows(resid_in, attn_gain)
    queries = jnp.dot(normed, full_query, preferred_element_type=jnp.float32).astype(jnp.bfloat16)
    new_keys = jnp.dot(normed, full_key, preferred_element_type=jnp.float32).astype(jnp.bfloat16)
    new_values = jnp.dot(normed, full_value, preferred_element_type=jnp.float32).astype(
        jnp.bfloat16
    )
    cache_count = cache.shape[0]
    split_cache = cache.reshape(cache_count, 2, head_group, HD)
    all_keys = jnp.concatenate(
        [split_cache[:, 0], new_keys.reshape(row_count, head_group, HD)], axis=0
    )
    all_values = jnp.concatenate(
        [split_cache[:, 1], new_values.reshape(row_count, head_group, HD)], axis=0
    )
    scores = jnp.einsum(
        "thc,rhc->htr",
        queries.reshape(row_count, head_group, HD),
        all_keys,
        preferred_element_type=jnp.float32,
    ) * HD ** (-0.5)
    valid_mask = key_masks(page_table[0], cache_len[0], new_len[0], row_count, PAGE)
    scores = jnp.where(valid_mask[None, :, :], scores, -1e30)
    highest = jnp.max(scores, axis=-1, keepdims=True)
    weights = jnp.exp(scores - highest)
    probs = (weights / jnp.sum(weights, axis=-1, keepdims=True)).astype(jnp.bfloat16)
    heads_out = (
        jnp.einsum("htr,rhc->thc", probs, all_values, preferred_element_type=jnp.float32)
        .astype(jnp.bfloat16)
        .reshape(row_count, head_group * HD)
    )
    attn_part = jnp.einsum("tc,dc->td", heads_out, full_out, preferred_element_type=jnp.float32)
    attn_out = dp_sum(attn_part.astype(jnp.bfloat16))
    residual = resid_in + attn_out
    moe_in = norm_rows(residual, moe_gain)
    kv_row = jnp.concatenate([new_keys, new_values], axis=1)
    kv_rank = route_rank(kv_owner, row_count, n_expert)[:, 0]
    kv_slot = kv_owner[:, 0] * kv_cap + kv_rank
    kv_pick = one_hot_rows(kv_slot[:, None], n_expert * kv_cap)
    kv_buffer = place_rows(kv_pick, kv_row).reshape(n_expert, kv_cap, kv_row.shape[1])
    slot_rank = route_rank(expert_ids, row_count, experts_all)
    tok_slot = expert_ids * capacity + slot_rank
    tok_pick = one_hot_rows(tok_slot, experts_all * capacity)
    tok_buffer = place_rows(tok_pick, moe_in).reshape(
        n_expert, local_experts, capacity, model_width
    )
    got_rows, got_kv = (
        lax.all_to_all(tok_buffer, "expert", split_axis=0, concat_axis=0, tiled=True),
        lax.all_to_all(kv_buffer, "expert", split_axis=0, concat_axis=0, tiled=True),
    )
    partial_value = expert_block(got_rows, w_gate, w_up, w_down)
    returned = lax.all_to_all(
        partial_value, "expert", split_axis=0, concat_axis=0, tiled=True
    ).reshape(experts_all, capacity, model_width)
    back_pick = (
        tok_slot.reshape(-1)[:, None] == jnp.arange(experts_all * capacity, dtype=jnp.int32)[None, :]
    ).astype(jnp.bfloat16)
    picked = (
        jnp.dot(
            back_pick,
            returned.reshape(experts_all * capacity, model_width),
            preferred_element_type=jnp.float32,
        )
        .astype(jnp.bfloat16)
        .astype(jnp.float32)
        .reshape(row_count, top_count, model_width)
    )
    moe_part = jnp.sum(picked * gate_weights[:, :, None], axis=1)
    moe_total = dp_sum(moe_part.astype(jnp.bfloat16))
    out = (residual + moe_total).astype(jnp.bfloat16)
    new_rows = got_kv.reshape(n_expert * kv_cap, kv_row.shape[1])
    return (out, new_rows)


def solution(mesh):
    placed = (
        P("expert", None),
        P(),
        P("expert", "dp"),
        P("expert", "dp"),
        P("expert", "dp"),
        P("expert", "dp"),
        P("expert", "dp"),
        P("expert", None),
        P("expert", None),
        P("expert", None),
        P("expert", None),
        P(),
        P("expert", None, "dp"),
        P("expert", None, "dp"),
        P("expert", "dp", None),
        P("expert", None),
        P("expert", None),
    )
    return jax.shard_map(
        local,
        mesh=mesh,
        in_specs=placed,
        out_specs=(P("expert", None), P("expert", "dp")),
        check_vma=False,
    )
```

```python
import jax
import jax.numpy as jnp
from jax import lax
from jax.sharding import PartitionSpec as P


HD = 128
PAGE = 128


EPSILON = 1e-05


def norm_rows(row_data, gain_vec):
    mean_sq = jnp.mean(row_data * row_data, axis=-1, keepdims=True)
    return (row_data * lax.rsqrt(mean_sq + EPSILON) * gain_vec).astype(jnp.bfloat16)


def route_rank(route_ids, block_rows, id_range):
    row_total = route_ids.shape[0]
    labels = jnp.arange(id_range, dtype=jnp.int32)
    counts = jnp.sum((route_ids[:, :, None] == labels[None, None, :]).astype(jnp.int32), axis=1)
    counts = counts.reshape(row_total // block_rows, block_rows, id_range)
    before = (jnp.cumsum(counts, axis=1) - counts).reshape(row_total, id_range)
    return jnp.take_along_axis(before, route_ids, axis=1)


def key_masks(table_row, cache_lens, new_lens, row_count, page_size):
    req_count = cache_lens.shape[0]
    pages_here = table_row.shape[0]
    per_request = pages_here // req_count
    slot_ids = jnp.arange(pages_here, dtype=jnp.int32)
    matches = (table_row[:, None] == slot_ids[None, :]).astype(jnp.int32)
    slot_of_page = jnp.sum(matches * slot_ids[:, None], axis=0)
    page_request = slot_of_page // per_request
    page_start = slot_of_page % per_request * page_size
    key_request = jnp.repeat(page_request, page_size)
    key_position = jnp.repeat(page_start, page_size) + jnp.tile(
        jnp.arange(page_size, dtype=jnp.int32), pages_here
    )
    request_ids = jnp.arange(req_count, dtype=jnp.int32)
    key_length = jnp.sum(
        (key_request[:, None] == request_ids[None, :]).astype(jnp.int32) * cache_lens[None, :],
        axis=1,
    )
    request_ends = jnp.cumsum(new_lens)
    tok_ids = jnp.arange(row_count, dtype=jnp.int32)
    tok_request = jnp.sum((tok_ids[:, None] >= request_ends[None, :]).astype(jnp.int32), axis=1)
    cached = (tok_request[:, None] == key_request[None, :]) & (key_position < key_length)[None, :]
    fresh_mask = tok_request[:, None] == tok_request[None, :]
    return jnp.concatenate([cached, fresh_mask], axis=1)


def dp_sum(part):
    n_dp = lax.axis_size("dp")
    me = lax.axis_index("dp")
    held = [part] + [
        lax.ppermute(part, "dp", [(i, (i + s) % n_dp) for i in range(n_dp)])
        for s in range(1, n_dp)
    ]
    held = jnp.stack(held).astype(jnp.float32)
    order = (me - jnp.arange(n_dp, dtype=jnp.int32)) % n_dp
    ordered = held[order]
    total = ordered[0]
    for j in range(1, n_dp):
        total = total + ordered[j]
    return total


def one_hot_rows(slots, slot_count):
    hits = slots[None, :, :] == jnp.arange(slot_count, dtype=jnp.int32)[:, None, None]
    return jnp.any(hits, axis=2).astype(jnp.bfloat16)


def place_rows(pick, rows):
    return jnp.dot(pick, rows, preferred_element_type=jnp.float32).astype(jnp.bfloat16)


def expert_block(routed, w_gate, w_up, w_down):
    n_dp = lax.axis_size("dp")
    sources, local_experts, slots, width = routed.shape
    held = [(jnp.stack([w_gate, w_up]), w_down)]
    for s in range(1, n_dp):
        pairs = [(i, (i + s) % n_dp) for i in range(n_dp)]
        held.append(tuple(lax.ppermute(a, "dp", pairs) for a in held[0]))
    outs = []
    for e in range(local_experts):
        rows = routed[:, e].reshape(sources * slots, width)
        total = None
        for gate_up, down in held:
            gate_proj = jnp.dot(rows, gate_up[0, e], preferred_element_type=jnp.float32)
            up_proj = jnp.dot(rows, gate_up[1, e], preferred_element_type=jnp.float32)
            active = (jax.nn.silu(gate_proj) * up_proj).astype(jnp.bfloat16)
            part = jnp.dot(active, down[e], preferred_element_type=jnp.float32)
            part = part.astype(jnp.bfloat16).astype(jnp.float32)
            total = part if total is None else total + part
        outs.append(total.reshape(sources, slots, width))
    return jnp.stack(outs, axis=1)


def local_body(
    tokens,
    attn_gain,
    w_query,
    w_key,
    w_value,
    w_out,
    cache,
    page_table,
    cache_len,
    new_len,
    kv_owner,
    moe_gain,
    w_gate,
    w_up,
    w_down,
    expert_ids,
    gate_weights,
):
    row_count, model_width = tokens.shape
    n_expert = lax.axis_size("expert")
    local_experts = w_gate.shape[0]
    experts_all = n_expert * local_experts
    top_count = expert_ids.shape[1]
    capacity = min(row_count, 2 * row_count * top_count // experts_all)
    kv_cap = max(2, 2 * row_count // n_expert)
    head_group = w_query.shape[1] // HD
    stacked = lax.all_gather(
        jnp.stack([w_query, w_key, w_value, w_out]), "expert", axis=1, tiled=True
    )
    full_query, full_key, full_value, full_out = (
        stacked[0],
        stacked[1],
        stacked[2],
        stacked[3],
    )
    resid_in = tokens.astype(jnp.float32)
    normed = norm_rows(resid_in, attn_gain)
    queries = jnp.dot(normed, full_query, preferred_element_type=jnp.float32).astype(jnp.bfloat16)
    new_keys = jnp.dot(normed, full_key, preferred_element_type=jnp.float32).astype(jnp.bfloat16)
    new_values = jnp.dot(normed, full_value, preferred_element_type=jnp.float32).astype(
        jnp.bfloat16
    )
    cache_count = cache.shape[0]
    split_cache = cache.reshape(cache_count, 2, head_group, HD)
    all_keys = jnp.concatenate(
        [split_cache[:, 0], new_keys.reshape(row_count, head_group, HD)], axis=0
    )
    all_values = jnp.concatenate(
        [split_cache[:, 1], new_values.reshape(row_count, head_group, HD)], axis=0
    )
    scores = jnp.einsum(
        "thc,rhc->htr",
        queries.reshape(row_count, head_group, HD),
        all_keys,
        preferred_element_type=jnp.float32,
    ) * HD ** (-0.5)
    valid_mask = key_masks(page_table[0], cache_len[0], new_len[0], row_count, PAGE)
    scores = jnp.where(valid_mask[None, :, :], scores, -1e30)
    highest = jnp.max(scores, axis=-1, keepdims=True)
    weights = jnp.exp(scores - highest)
    probs = (weights / jnp.sum(weights, axis=-1, keepdims=True)).astype(jnp.bfloat16)
    heads_out = (
        jnp.einsum("htr,rhc->thc", probs, all_values, preferred_element_type=jnp.float32)
        .astype(jnp.bfloat16)
        .reshape(row_count, head_group * HD)
    )
    attn_part = jnp.einsum("tc,dc->td", heads_out, full_out, preferred_element_type=jnp.float32)
    attn_out = dp_sum(attn_part.astype(jnp.bfloat16))
    residual = resid_in + attn_out
    moe_in = norm_rows(residual, moe_gain)
    kv_row = jnp.concatenate([new_keys, new_values], axis=1)
    kv_rank = route_rank(kv_owner, row_count, n_expert)[:, 0]
    kv_slot = kv_owner[:, 0] * kv_cap + kv_rank
    kv_pick = one_hot_rows(kv_slot[:, None], n_expert * kv_cap)
    kv_buffer = place_rows(kv_pick, kv_row).reshape(n_expert, kv_cap, kv_row.shape[1])
    n_dp = lax.axis_size("dp")
    me_dp = lax.axis_index("dp")
    quarter = capacity // n_dp
    slot_rank = route_rank(expert_ids, row_count, experts_all)
    in_quarter = slot_rank // quarter == me_dp
    q_slot = jnp.where(in_quarter, expert_ids * quarter + slot_rank % quarter, -1)
    tok_pick = one_hot_rows(q_slot, experts_all * quarter)
    tok_buffer = place_rows(tok_pick, moe_in).reshape(
        n_expert, local_experts, quarter, model_width
    )
    got_rows = lax.all_to_all(tok_buffer, "expert", split_axis=0, concat_axis=0, tiled=True)
    got_kv = lax.all_to_all(kv_buffer, "expert", split_axis=0, concat_axis=0, tiled=True)
    contrib = expert_block(got_rows, w_gate, w_up, w_down)
    returned = lax.all_to_all(
        contrib.astype(jnp.bfloat16), "expert", split_axis=0, concat_axis=0, tiled=True
    ).reshape(experts_all * quarter, model_width)
    back_pick = (
        q_slot.reshape(-1)[:, None]
        == jnp.arange(experts_all * quarter, dtype=jnp.int32)[None, :]
    ).astype(jnp.bfloat16)
    picked = jnp.dot(back_pick, returned, preferred_element_type=jnp.float32).reshape(
        row_count, top_count, model_width
    )
    moe_part = jnp.sum(picked * gate_weights[:, :, None], axis=1)
    moe_total = dp_sum(moe_part.astype(jnp.bfloat16))
    out = (residual + moe_total).astype(jnp.bfloat16)
    new_rows = got_kv.reshape(n_expert * kv_cap, kv_row.shape[1])
    return (out, new_rows)


def solution(mesh):
    placed = (
        P("expert", None),
        P(),
        P("expert", "dp"),
        P("expert", "dp"),
        P("expert", "dp"),
        P("expert", "dp"),
        P("expert", "dp"),
        P("expert", None),
        P("expert", None),
        P("expert", None),
        P("expert", None),
        P(),
        P("expert", None, "dp"),
        P("expert", None, "dp"),
        P("expert", "dp", None),
        P("expert", None),
        P("expert", None),
    )
    return jax.shard_map(
        local_body,
        mesh=mesh,
        in_specs=placed,
        out_specs=(P("expert", None), P("expert", "dp")),
        check_vma=False,
    )
```

```python
import jax
import jax.numpy as jnp
from jax import lax
from jax.sharding import PartitionSpec as P


HD = 128
PAGE = 128


EPSILON = 1e-05


def norm_rows(row_data, gain_vec):
    mean_sq = jnp.mean(row_data * row_data, axis=-1, keepdims=True)
    return (row_data * lax.rsqrt(mean_sq + EPSILON) * gain_vec).astype(jnp.bfloat16)


def route_rank(route_ids, block_rows, id_range):
    row_total = route_ids.shape[0]
    labels = jnp.arange(id_range, dtype=jnp.int32)
    counts = jnp.sum((route_ids[:, :, None] == labels[None, None, :]).astype(jnp.int32), axis=1)
    counts = counts.reshape(row_total // block_rows, block_rows, id_range)
    before = (jnp.cumsum(counts, axis=1) - counts).reshape(row_total, id_range)
    return jnp.take_along_axis(before, route_ids, axis=1)


def key_masks(table_row, cache_lens, new_lens, row_count, page_size):
    req_count = cache_lens.shape[0]
    pages_here = table_row.shape[0]
    per_request = pages_here // req_count
    slot_ids = jnp.arange(pages_here, dtype=jnp.int32)
    matches = (table_row[:, None] == slot_ids[None, :]).astype(jnp.int32)
    slot_of_page = jnp.sum(matches * slot_ids[:, None], axis=0)
    page_request = slot_of_page // per_request
    page_start = slot_of_page % per_request * page_size
    key_request = jnp.repeat(page_request, page_size)
    key_position = jnp.repeat(page_start, page_size) + jnp.tile(
        jnp.arange(page_size, dtype=jnp.int32), pages_here
    )
    request_ids = jnp.arange(req_count, dtype=jnp.int32)
    key_length = jnp.sum(
        (key_request[:, None] == request_ids[None, :]).astype(jnp.int32) * cache_lens[None, :],
        axis=1,
    )
    request_ends = jnp.cumsum(new_lens)
    tok_ids = jnp.arange(row_count, dtype=jnp.int32)
    tok_request = jnp.sum((tok_ids[:, None] >= request_ends[None, :]).astype(jnp.int32), axis=1)
    cached = (tok_request[:, None] == key_request[None, :]) & (key_position < key_length)[None, :]
    fresh_mask = tok_request[:, None] == tok_request[None, :]
    return jnp.concatenate([cached, fresh_mask], axis=1)


def dp_sum(part):
    n_dp = lax.axis_size("dp")
    me = lax.axis_index("dp")
    held = [part] + [
        lax.ppermute(part, "dp", [(i, (i + s) % n_dp) for i in range(n_dp)])
        for s in range(1, n_dp)
    ]
    held = jnp.stack(held).astype(jnp.float32)
    order = (me - jnp.arange(n_dp, dtype=jnp.int32)) % n_dp
    ordered = held[order]
    total = ordered[0]
    for j in range(1, n_dp):
        total = total + ordered[j]
    return total


def one_hot_rows(slots, slot_count):
    hits = slots[None, :, :] == jnp.arange(slot_count, dtype=jnp.int32)[:, None, None]
    return jnp.any(hits, axis=2).astype(jnp.bfloat16)


def place_rows(pick, rows):
    return jnp.dot(pick, rows, preferred_element_type=jnp.float32).astype(jnp.bfloat16)


def expert_block(routed, w_gate, w_up, w_down):
    n_dp = lax.axis_size("dp")
    sources, local_experts, slots, width = routed.shape
    me_dp = lax.axis_index("dp")
    down_all = lax.all_gather(w_down, "dp", axis=0, tiled=False)
    held = [(jnp.stack([w_gate, w_up]), w_down)]
    for s in range(1, n_dp):
        pairs = [(i, (i + s) % n_dp) for i in range(n_dp)]
        gate_up = lax.ppermute(held[0][0], "dp", pairs)
        down = lax.dynamic_index_in_dim(down_all, (me_dp - s) % n_dp, 0, keepdims=False)
        held.append((gate_up, down))
    outs = []
    for e in range(local_experts):
        rows = routed[:, e].reshape(sources * slots, width)
        total = None
        for gate_up, down in held:
            gate_proj = jnp.dot(rows, gate_up[0, e], preferred_element_type=jnp.float32)
            up_proj = jnp.dot(rows, gate_up[1, e], preferred_element_type=jnp.float32)
            active = (jax.nn.silu(gate_proj) * up_proj).astype(jnp.bfloat16)
            part = jnp.dot(active, down[e], preferred_element_type=jnp.float32)
            part = part.astype(jnp.bfloat16).astype(jnp.float32)
            total = part if total is None else total + part
        outs.append(total.reshape(sources, slots, width))
    return jnp.stack(outs, axis=1)


def local_body(
    tokens,
    attn_gain,
    w_query,
    w_key,
    w_value,
    w_out,
    cache,
    page_table,
    cache_len,
    new_len,
    kv_owner,
    moe_gain,
    w_gate,
    w_up,
    w_down,
    expert_ids,
    gate_weights,
):
    row_count, model_width = tokens.shape
    n_expert = lax.axis_size("expert")
    local_experts = w_gate.shape[0]
    experts_all = n_expert * local_experts
    top_count = expert_ids.shape[1]
    capacity = min(row_count, 2 * row_count * top_count // experts_all)
    kv_cap = max(2, 2 * row_count // n_expert)
    head_group = w_query.shape[1] // HD
    stacked = lax.all_gather(
        jnp.stack([w_query, w_key, w_value, w_out]), "expert", axis=1, tiled=True
    )
    full_query, full_key, full_value, full_out = (
        stacked[0],
        stacked[1],
        stacked[2],
        stacked[3],
    )
    resid_in = tokens.astype(jnp.float32)
    normed = norm_rows(resid_in, attn_gain)
    queries = jnp.dot(normed, full_query, preferred_element_type=jnp.float32).astype(jnp.bfloat16)
    new_keys = jnp.dot(normed, full_key, preferred_element_type=jnp.float32).astype(jnp.bfloat16)
    new_values = jnp.dot(normed, full_value, preferred_element_type=jnp.float32).astype(
        jnp.bfloat16
    )
    cache_count = cache.shape[0]
    split_cache = cache.reshape(cache_count, 2, head_group, HD)
    all_keys = jnp.concatenate(
        [split_cache[:, 0], new_keys.reshape(row_count, head_group, HD)], axis=0
    )
    all_values = jnp.concatenate(
        [split_cache[:, 1], new_values.reshape(row_count, head_group, HD)], axis=0
    )
    scores = jnp.einsum(
        "thc,rhc->htr",
        queries.reshape(row_count, head_group, HD),
        all_keys,
        preferred_element_type=jnp.float32,
    ) * HD ** (-0.5)
    valid_mask = key_masks(page_table[0], cache_len[0], new_len[0], row_count, PAGE)
    scores = jnp.where(valid_mask[None, :, :], scores, -1e30)
    highest = jnp.max(scores, axis=-1, keepdims=True)
    weights = jnp.exp(scores - highest)
    probs = (weights / jnp.sum(weights, axis=-1, keepdims=True)).astype(jnp.bfloat16)
    heads_out = (
        jnp.einsum("htr,rhc->thc", probs, all_values, preferred_element_type=jnp.float32)
        .astype(jnp.bfloat16)
        .reshape(row_count, head_group * HD)
    )
    attn_part = jnp.einsum("tc,dc->td", heads_out, full_out, preferred_element_type=jnp.float32)
    attn_out = dp_sum(attn_part.astype(jnp.bfloat16))
    residual = resid_in + attn_out
    moe_in = norm_rows(residual, moe_gain)
    kv_row = jnp.concatenate([new_keys, new_values], axis=1)
    kv_rank = route_rank(kv_owner, row_count, n_expert)[:, 0]
    kv_slot = kv_owner[:, 0] * kv_cap + kv_rank
    kv_pick = one_hot_rows(kv_slot[:, None], n_expert * kv_cap)
    kv_buffer = place_rows(kv_pick, kv_row).reshape(n_expert, kv_cap, kv_row.shape[1])
    n_dp = lax.axis_size("dp")
    me_dp = lax.axis_index("dp")
    quarter = capacity // n_dp
    slot_rank = route_rank(expert_ids, row_count, experts_all)
    in_quarter = slot_rank // quarter == me_dp
    q_slot = jnp.where(in_quarter, expert_ids * quarter + slot_rank % quarter, -1)
    tok_pick = one_hot_rows(q_slot, experts_all * quarter)
    tok_buffer = place_rows(tok_pick, moe_in).reshape(
        n_expert, local_experts, quarter, model_width
    )
    kv_width = kv_cap * kv_row.shape[1]
    if kv_width == model_width and local_experts == 1:
        send = jnp.concatenate(
            [tok_buffer, kv_buffer.reshape(n_expert, 1, 1, model_width)], axis=2
        )
        got = lax.all_to_all(send, "expert", split_axis=0, concat_axis=0, tiled=True)
        got_rows = got[:, :, :quarter]
        got_kv = got[:, 0, quarter].reshape(n_expert, kv_cap, kv_row.shape[1])
    else:
        got_rows = lax.all_to_all(tok_buffer, "expert", split_axis=0, concat_axis=0, tiled=True)
        got_kv = lax.all_to_all(kv_buffer, "expert", split_axis=0, concat_axis=0, tiled=True)
    contrib = expert_block(got_rows, w_gate, w_up, w_down)
    returned = lax.all_to_all(
        contrib.astype(jnp.bfloat16), "expert", split_axis=0, concat_axis=0, tiled=True
    ).reshape(experts_all * quarter, model_width)
    back_pick = (
        q_slot.reshape(-1)[:, None]
        == jnp.arange(experts_all * quarter, dtype=jnp.int32)[None, :]
    ).astype(jnp.bfloat16)
    picked = jnp.dot(back_pick, returned, preferred_element_type=jnp.float32).reshape(
        row_count, top_count, model_width
    )
    moe_part = jnp.sum(picked * gate_weights[:, :, None], axis=1)
    moe_total = dp_sum(moe_part.astype(jnp.bfloat16))
    out = (residual + moe_total).astype(jnp.bfloat16)
    new_rows = got_kv.reshape(n_expert * kv_cap, kv_row.shape[1])
    return (out, new_rows)


def solution(mesh):
    placed = (
        P("expert", None),
        P(),
        P("expert", "dp"),
        P("expert", "dp"),
        P("expert", "dp"),
        P("expert", "dp"),
        P("expert", "dp"),
        P("expert", None),
        P("expert", None),
        P("expert", None),
        P("expert", None),
        P(),
        P("expert", None, "dp"),
        P("expert", None, "dp"),
        P("expert", "dp", None),
        P("expert", None),
        P("expert", None),
    )
    return jax.shard_map(
        local_body,
        mesh=mesh,
        in_specs=placed,
        out_specs=(P("expert", None), P("expert", "dp")),
        check_vma=False,
    )
```

```python
import jax
import jax.numpy as jnp
from jax import lax
from jax.sharding import PartitionSpec as P


HD = 128
PAGE = 128


EPSILON = 1e-05


def norm_rows(row_data, gain_vec):
    mean_sq = jnp.mean(row_data * row_data, axis=-1, keepdims=True)
    return (row_data * lax.rsqrt(mean_sq + EPSILON) * gain_vec).astype(jnp.bfloat16)


def route_rank(route_ids, block_rows, id_range):
    row_total = route_ids.shape[0]
    labels = jnp.arange(id_range, dtype=jnp.int32)
    counts = jnp.sum((route_ids[:, :, None] == labels[None, None, :]).astype(jnp.int32), axis=1)
    counts = counts.reshape(row_total // block_rows, block_rows, id_range)
    before = (jnp.cumsum(counts, axis=1) - counts).reshape(row_total, id_range)
    return jnp.take_along_axis(before, route_ids, axis=1)


def key_masks(table_row, cache_lens, new_lens, row_count, page_size):
    req_count = cache_lens.shape[0]
    pages_here = table_row.shape[0]
    per_request = pages_here // req_count
    slot_ids = jnp.arange(pages_here, dtype=jnp.int32)
    matches = (table_row[:, None] == slot_ids[None, :]).astype(jnp.int32)
    slot_of_page = jnp.sum(matches * slot_ids[:, None], axis=0)
    page_request = slot_of_page // per_request
    page_start = slot_of_page % per_request * page_size
    key_request = jnp.repeat(page_request, page_size)
    key_position = jnp.repeat(page_start, page_size) + jnp.tile(
        jnp.arange(page_size, dtype=jnp.int32), pages_here
    )
    request_ids = jnp.arange(req_count, dtype=jnp.int32)
    key_length = jnp.sum(
        (key_request[:, None] == request_ids[None, :]).astype(jnp.int32) * cache_lens[None, :],
        axis=1,
    )
    request_ends = jnp.cumsum(new_lens)
    tok_ids = jnp.arange(row_count, dtype=jnp.int32)
    tok_request = jnp.sum((tok_ids[:, None] >= request_ends[None, :]).astype(jnp.int32), axis=1)
    cached = (tok_request[:, None] == key_request[None, :]) & (key_position < key_length)[None, :]
    fresh_mask = tok_request[:, None] == tok_request[None, :]
    return jnp.concatenate([cached, fresh_mask], axis=1)


def dp_sum(part):
    n_dp = lax.axis_size("dp")
    me = lax.axis_index("dp")
    held = [part] + [
        lax.ppermute(part, "dp", [(i, (i + s) % n_dp) for i in range(n_dp)])
        for s in range(1, n_dp)
    ]
    held = jnp.stack(held).astype(jnp.float32)
    order = (me - jnp.arange(n_dp, dtype=jnp.int32)) % n_dp
    ordered = held[order]
    total = ordered[0]
    for j in range(1, n_dp):
        total = total + ordered[j]
    return total


def one_hot_rows(slots, slot_count):
    hits = slots[None, :, :] == jnp.arange(slot_count, dtype=jnp.int32)[:, None, None]
    return jnp.any(hits, axis=2).astype(jnp.bfloat16)


def place_rows(pick, rows):
    return jnp.dot(pick, rows, preferred_element_type=jnp.float32).astype(jnp.bfloat16)


def expert_block(routed, w_gate, w_up, w_down):
    n_dp = lax.axis_size("dp")
    sources, local_experts, slots, width = routed.shape
    held = [(jnp.stack([w_gate, w_up]), w_down)]
    for s in range(1, n_dp):
        pairs = [(i, (i + s) % n_dp) for i in range(n_dp)]
        gate_up = lax.ppermute(held[0][0], "dp", pairs)
        down = lax.ppermute(held[0][1], "dp", pairs)
        held.append((gate_up, down))
    outs = []
    for e in range(local_experts):
        rows = routed[:, e].reshape(sources * slots, width)
        total = None
        for gate_up, down in held:
            gate_proj = jnp.dot(rows, gate_up[0, e], preferred_element_type=jnp.float32)
            up_proj = jnp.dot(rows, gate_up[1, e], preferred_element_type=jnp.float32)
            active = (jax.nn.silu(gate_proj) * up_proj).astype(jnp.bfloat16)
            part = jnp.dot(active, down[e], preferred_element_type=jnp.float32)
            part = part.astype(jnp.bfloat16).astype(jnp.float32)
            total = part if total is None else total + part
        outs.append(total.reshape(sources, slots, width))
    return jnp.stack(outs, axis=1)


def local_body(
    tokens,
    attn_gain,
    w_query,
    w_key,
    w_value,
    w_out,
    cache,
    page_table,
    cache_len,
    new_len,
    kv_owner,
    moe_gain,
    w_gate,
    w_up,
    w_down,
    expert_ids,
    gate_weights,
):
    row_count, model_width = tokens.shape
    n_expert = lax.axis_size("expert")
    local_experts = w_gate.shape[0]
    experts_all = n_expert * local_experts
    top_count = expert_ids.shape[1]
    capacity = min(row_count, 2 * row_count * top_count // experts_all)
    kv_cap = max(2, 2 * row_count // n_expert)
    head_group = w_query.shape[1] // HD
    stacked = lax.all_gather(
        jnp.stack([w_query, w_key, w_value, w_out]), "expert", axis=1, tiled=True
    )
    full_query, full_key, full_value, full_out = (
        stacked[0],
        stacked[1],
        stacked[2],
        stacked[3],
    )
    resid_in = tokens.astype(jnp.float32)
    normed = norm_rows(resid_in, attn_gain)
    queries = jnp.dot(normed, full_query, preferred_element_type=jnp.float32).astype(jnp.bfloat16)
    new_keys = jnp.dot(normed, full_key, preferred_element_type=jnp.float32).astype(jnp.bfloat16)
    new_values = jnp.dot(normed, full_value, preferred_element_type=jnp.float32).astype(
        jnp.bfloat16
    )
    cache_count = cache.shape[0]
    split_cache = cache.reshape(cache_count, 2, head_group, HD)
    all_keys = jnp.concatenate(
        [split_cache[:, 0], new_keys.reshape(row_count, head_group, HD)], axis=0
    )
    all_values = jnp.concatenate(
        [split_cache[:, 1], new_values.reshape(row_count, head_group, HD)], axis=0
    )
    scores = jnp.einsum(
        "thc,rhc->htr",
        queries.reshape(row_count, head_group, HD),
        all_keys,
        preferred_element_type=jnp.float32,
    ) * HD ** (-0.5)
    valid_mask = key_masks(page_table[0], cache_len[0], new_len[0], row_count, PAGE)
    scores = jnp.where(valid_mask[None, :, :], scores, -1e30)
    highest = jnp.max(scores, axis=-1, keepdims=True)
    weights = jnp.exp(scores - highest)
    probs = (weights / jnp.sum(weights, axis=-1, keepdims=True)).astype(jnp.bfloat16)
    heads_out = (
        jnp.einsum("htr,rhc->thc", probs, all_values, preferred_element_type=jnp.float32)
        .astype(jnp.bfloat16)
        .reshape(row_count, head_group * HD)
    )
    attn_part = jnp.einsum("tc,dc->td", heads_out, full_out, preferred_element_type=jnp.float32)
    attn_out = dp_sum(attn_part.astype(jnp.bfloat16))
    residual = resid_in + attn_out
    moe_in = norm_rows(residual, moe_gain)
    kv_row = jnp.concatenate([new_keys, new_values], axis=1)
    kv_rank = route_rank(kv_owner, row_count, n_expert)[:, 0]
    kv_slot = kv_owner[:, 0] * kv_cap + kv_rank
    kv_pick = one_hot_rows(kv_slot[:, None], n_expert * kv_cap)
    kv_buffer = place_rows(kv_pick, kv_row).reshape(n_expert, kv_cap, kv_row.shape[1])
    n_dp = lax.axis_size("dp")
    me_dp = lax.axis_index("dp")
    quarter = capacity // n_dp
    slot_rank = route_rank(expert_ids, row_count, experts_all)
    in_quarter = slot_rank // quarter == me_dp
    q_slot = jnp.where(in_quarter, expert_ids * quarter + slot_rank % quarter, -1)
    tok_pick = one_hot_rows(q_slot, experts_all * quarter)
    tok_buffer = place_rows(tok_pick, moe_in).reshape(
        n_expert, local_experts, quarter, model_width
    )
    kv_width = kv_cap * kv_row.shape[1]
    if kv_width == model_width and local_experts == 1 and (quarter + 1) * model_width % 2048 == 0:
        send = jnp.concatenate(
            [tok_buffer, kv_buffer.reshape(n_expert, 1, 1, model_width)], axis=2
        )
        flat = (quarter + 1) * model_width
        got = lax.all_to_all(
            send.reshape(n_expert, flat // 128, 128), "expert", split_axis=0, concat_axis=0, tiled=True
        ).reshape(n_expert, 1, quarter + 1, model_width)
        got_rows = got[:, :, :quarter]
        got_kv = got[:, 0, quarter].reshape(n_expert, kv_cap, kv_row.shape[1])
    else:
        got_rows = lax.all_to_all(tok_buffer, "expert", split_axis=0, concat_axis=0, tiled=True)
        got_kv = lax.all_to_all(kv_buffer, "expert", split_axis=0, concat_axis=0, tiled=True)
    contrib = expert_block(got_rows, w_gate, w_up, w_down)
    returned = lax.all_to_all(
        contrib.astype(jnp.bfloat16), "expert", split_axis=0, concat_axis=0, tiled=True
    ).reshape(experts_all * quarter, model_width)
    back_pick = (
        q_slot.reshape(-1)[:, None]
        == jnp.arange(experts_all * quarter, dtype=jnp.int32)[None, :]
    ).astype(jnp.bfloat16)
    picked = jnp.dot(back_pick, returned, preferred_element_type=jnp.float32).reshape(
        row_count, top_count, model_width
    )
    moe_part = jnp.sum(picked * gate_weights[:, :, None], axis=1)
    moe_total = dp_sum(moe_part.astype(jnp.bfloat16))
    out = (residual + moe_total).astype(jnp.bfloat16)
    new_rows = got_kv.reshape(n_expert * kv_cap, kv_row.shape[1])
    return (out, new_rows)


def solution(mesh):
    placed = (
        P("expert", None),
        P(),
        P("expert", "dp"),
        P("expert", "dp"),
        P("expert", "dp"),
        P("expert", "dp"),
        P("expert", "dp"),
        P("expert", None),
        P("expert", None),
        P("expert", None),
        P("expert", None),
        P(),
        P("expert", None, "dp"),
        P("expert", None, "dp"),
        P("expert", "dp", None),
        P("expert", None),
        P("expert", None),
    )
    return jax.shard_map(
        local_body,
        mesh=mesh,
        in_specs=placed,
        out_specs=(P("expert", None), P("expert", "dp")),
        check_vma=False,
    )
```

```python
import jax
import jax.numpy as jnp
from jax import lax
from jax.sharding import PartitionSpec as P


HD = 128
PAGE = 128


EPSILON = 1e-05


def norm_rows(row_data, gain_vec):
    mean_sq = jnp.mean(row_data * row_data, axis=-1, keepdims=True)
    return (row_data * lax.rsqrt(mean_sq + EPSILON) * gain_vec).astype(jnp.bfloat16)


def route_rank(route_ids, block_rows, id_range):
    row_total = route_ids.shape[0]
    labels = jnp.arange(id_range, dtype=jnp.int32)
    counts = jnp.sum((route_ids[:, :, None] == labels[None, None, :]).astype(jnp.int32), axis=1)
    counts = counts.reshape(row_total // block_rows, block_rows, id_range)
    before = (jnp.cumsum(counts, axis=1) - counts).reshape(row_total, id_range)
    return jnp.take_along_axis(before, route_ids, axis=1)


def key_masks(table_row, cache_lens, new_lens, row_count, page_size):
    req_count = cache_lens.shape[0]
    pages_here = table_row.shape[0]
    per_request = pages_here // req_count
    slot_ids = jnp.arange(pages_here, dtype=jnp.int32)
    matches = (table_row[:, None] == slot_ids[None, :]).astype(jnp.int32)
    slot_of_page = jnp.sum(matches * slot_ids[:, None], axis=0)
    page_request = slot_of_page // per_request
    page_start = slot_of_page % per_request * page_size
    key_request = jnp.repeat(page_request, page_size)
    key_position = jnp.repeat(page_start, page_size) + jnp.tile(
        jnp.arange(page_size, dtype=jnp.int32), pages_here
    )
    request_ids = jnp.arange(req_count, dtype=jnp.int32)
    key_length = jnp.sum(
        (key_request[:, None] == request_ids[None, :]).astype(jnp.int32) * cache_lens[None, :],
        axis=1,
    )
    request_ends = jnp.cumsum(new_lens)
    tok_ids = jnp.arange(row_count, dtype=jnp.int32)
    tok_request = jnp.sum((tok_ids[:, None] >= request_ends[None, :]).astype(jnp.int32), axis=1)
    cached = (tok_request[:, None] == key_request[None, :]) & (key_position < key_length)[None, :]
    fresh_mask = tok_request[:, None] == tok_request[None, :]
    return jnp.concatenate([cached, fresh_mask], axis=1)


def dp_sum(part):
    n_dp = lax.axis_size("dp")
    me = lax.axis_index("dp")
    held = [part] + [
        lax.ppermute(part, "dp", [(i, (i + s) % n_dp) for i in range(n_dp)])
        for s in range(1, n_dp)
    ]
    total = None
    for j in range(n_dp):
        term = lax.select_n((me - j) % n_dp, *held).astype(jnp.float32)
        total = term if total is None else total + term
    return total


def one_hot_rows(slots, slot_count):
    hits = slots[None, :, :] == jnp.arange(slot_count, dtype=jnp.int32)[:, None, None]
    return jnp.any(hits, axis=2).astype(jnp.bfloat16)


def place_rows(pick, rows):
    return jnp.dot(pick, rows, preferred_element_type=jnp.float32).astype(jnp.bfloat16)


def expert_block(routed, w_gate, w_up, w_down):
    n_dp = lax.axis_size("dp")
    sources, local_experts, slots, width = routed.shape
    held = [(jnp.stack([w_gate, w_up]), w_down)]
    for s in range(1, n_dp):
        pairs = [(i, (i + s) % n_dp) for i in range(n_dp)]
        gate_up = lax.ppermute(held[0][0], "dp", pairs)
        down = lax.ppermute(held[0][1], "dp", pairs)
        held.append((gate_up, down))
    outs = []
    for e in range(local_experts):
        rows = routed[:, e].reshape(sources * slots, width)
        total = None
        for gate_up, down in held:
            gate_proj = jnp.dot(rows, gate_up[0, e], preferred_element_type=jnp.float32)
            up_proj = jnp.dot(rows, gate_up[1, e], preferred_element_type=jnp.float32)
            active = (jax.nn.silu(gate_proj) * up_proj).astype(jnp.bfloat16)
            part = jnp.dot(active, down[e], preferred_element_type=jnp.float32)
            part = part.astype(jnp.bfloat16).astype(jnp.float32)
            total = part if total is None else total + part
        outs.append(total.reshape(sources, slots, width))
    return jnp.stack(outs, axis=1)


def local_body(
    tokens,
    attn_gain,
    w_query,
    w_key,
    w_value,
    w_out,
    cache,
    page_table,
    cache_len,
    new_len,
    kv_owner,
    moe_gain,
    w_gate,
    w_up,
    w_down,
    expert_ids,
    gate_weights,
):
    row_count, model_width = tokens.shape
    n_expert = lax.axis_size("expert")
    local_experts = w_gate.shape[0]
    experts_all = n_expert * local_experts
    top_count = expert_ids.shape[1]
    capacity = min(row_count, 2 * row_count * top_count // experts_all)
    kv_cap = max(2, 2 * row_count // n_expert)
    head_group = w_query.shape[1] // HD
    stacked = lax.all_gather(
        jnp.stack([w_query, w_key, w_value, w_out]), "expert", axis=1, tiled=True
    )
    full_query, full_key, full_value, full_out = (
        stacked[0],
        stacked[1],
        stacked[2],
        stacked[3],
    )
    resid_in = tokens.astype(jnp.float32)
    normed = norm_rows(resid_in, attn_gain)
    queries = jnp.dot(normed, full_query, preferred_element_type=jnp.float32).astype(jnp.bfloat16)
    new_keys = jnp.dot(normed, full_key, preferred_element_type=jnp.float32).astype(jnp.bfloat16)
    new_values = jnp.dot(normed, full_value, preferred_element_type=jnp.float32).astype(
        jnp.bfloat16
    )
    cache_count = cache.shape[0]
    split_cache = cache.reshape(cache_count, 2, head_group, HD)
    all_keys = jnp.concatenate(
        [split_cache[:, 0], new_keys.reshape(row_count, head_group, HD)], axis=0
    )
    all_values = jnp.concatenate(
        [split_cache[:, 1], new_values.reshape(row_count, head_group, HD)], axis=0
    )
    scores = jnp.einsum(
        "thc,rhc->htr",
        queries.reshape(row_count, head_group, HD),
        all_keys,
        preferred_element_type=jnp.float32,
    ) * HD ** (-0.5)
    valid_mask = key_masks(page_table[0], cache_len[0], new_len[0], row_count, PAGE)
    scores = jnp.where(valid_mask[None, :, :], scores, -1e30)
    highest = jnp.max(scores, axis=-1, keepdims=True)
    weights = jnp.exp(scores - highest)
    probs = (weights / jnp.sum(weights, axis=-1, keepdims=True)).astype(jnp.bfloat16)
    heads_out = (
        jnp.einsum("htr,rhc->thc", probs, all_values, preferred_element_type=jnp.float32)
        .astype(jnp.bfloat16)
        .reshape(row_count, head_group * HD)
    )
    attn_part = jnp.einsum("tc,dc->td", heads_out, full_out, preferred_element_type=jnp.float32)
    attn_out = dp_sum(attn_part.astype(jnp.bfloat16))
    residual = resid_in + attn_out
    moe_in = norm_rows(residual, moe_gain)
    kv_row = jnp.concatenate([new_keys, new_values], axis=1)
    kv_rank = route_rank(kv_owner, row_count, n_expert)[:, 0]
    kv_slot = kv_owner[:, 0] * kv_cap + kv_rank
    kv_pick = one_hot_rows(kv_slot[:, None], n_expert * kv_cap)
    kv_buffer = place_rows(kv_pick, kv_row).reshape(n_expert, kv_cap, kv_row.shape[1])
    n_dp = lax.axis_size("dp")
    me_dp = lax.axis_index("dp")
    quarter = capacity // n_dp
    slot_rank = route_rank(expert_ids, row_count, experts_all)
    in_quarter = slot_rank // quarter == me_dp
    q_slot = jnp.where(in_quarter, expert_ids * quarter + slot_rank % quarter, -1)
    tok_pick = one_hot_rows(q_slot, experts_all * quarter)
    tok_buffer = place_rows(tok_pick, moe_in).reshape(
        n_expert, local_experts, quarter, model_width
    )
    kv_width = kv_cap * kv_row.shape[1]
    extra = kv_width // quarter
    if local_experts == 1 and kv_width % quarter == 0 and extra % 128 == 0:
        send = jnp.concatenate(
            [tok_buffer, kv_buffer.reshape(n_expert, 1, quarter, extra)], axis=3
        )
        got = lax.all_to_all(send, "expert", split_axis=0, concat_axis=0, tiled=True)
        got_rows = got[:, :, :, :model_width]
        got_kv = got[:, :, :, model_width:].reshape(n_expert, kv_cap, kv_row.shape[1])
    else:
        got_rows = lax.all_to_all(tok_buffer, "expert", split_axis=0, concat_axis=0, tiled=True)
        got_kv = lax.all_to_all(kv_buffer, "expert", split_axis=0, concat_axis=0, tiled=True)
    contrib = expert_block(got_rows, w_gate, w_up, w_down)
    returned = lax.all_to_all(
        contrib.astype(jnp.bfloat16), "expert", split_axis=0, concat_axis=0, tiled=True
    ).reshape(experts_all * quarter, model_width)
    back_pick = (
        q_slot.reshape(-1)[:, None]
        == jnp.arange(experts_all * quarter, dtype=jnp.int32)[None, :]
    ).astype(jnp.bfloat16)
    picked = jnp.dot(back_pick, returned, preferred_element_type=jnp.float32).reshape(
        row_count, top_count, model_width
    )
    moe_part = jnp.sum(picked * gate_weights[:, :, None], axis=1)
    moe_total = dp_sum(moe_part.astype(jnp.bfloat16))
    out = (residual + moe_total).astype(jnp.bfloat16)
    new_rows = got_kv.reshape(n_expert * kv_cap, kv_row.shape[1])
    return (out, new_rows)


def solution(mesh):
    placed = (
        P("expert", None),
        P(),
        P("expert", "dp"),
        P("expert", "dp"),
        P("expert", "dp"),
        P("expert", "dp"),
        P("expert", "dp"),
        P("expert", None),
        P("expert", None),
        P("expert", None),
        P("expert", None),
        P(),
        P("expert", None, "dp"),
        P("expert", None, "dp"),
        P("expert", "dp", None),
        P("expert", None),
        P("expert", None),
    )
    return jax.shard_map(
        local_body,
        mesh=mesh,
        in_specs=placed,
        out_specs=(P("expert", None), P("expert", "dp")),
        check_vma=False,
    )
```

```python
import jax
import jax.numpy as jnp
from jax import lax
from jax.sharding import PartitionSpec as P


HD = 128
PAGE = 128


EPSILON = 1e-05


def norm_rows(row_data, gain_vec):
    mean_sq = jnp.mean(row_data * row_data, axis=-1, keepdims=True)
    return (row_data * lax.rsqrt(mean_sq + EPSILON) * gain_vec).astype(jnp.bfloat16)


def route_rank(route_ids, block_rows, id_range):
    row_total = route_ids.shape[0]
    labels = jnp.arange(id_range, dtype=jnp.int32)
    counts = jnp.sum((route_ids[:, :, None] == labels[None, None, :]).astype(jnp.int32), axis=1)
    counts = counts.reshape(row_total // block_rows, block_rows, id_range)
    before = (jnp.cumsum(counts, axis=1) - counts).reshape(row_total, id_range)
    return jnp.take_along_axis(before, route_ids, axis=1)


def key_masks(table_row, cache_lens, new_lens, row_count, page_size):
    req_count = cache_lens.shape[0]
    pages_here = table_row.shape[0]
    per_request = pages_here // req_count
    slot_ids = jnp.arange(pages_here, dtype=jnp.int32)
    matches = (table_row[:, None] == slot_ids[None, :]).astype(jnp.int32)
    slot_of_page = jnp.sum(matches * slot_ids[:, None], axis=0)
    page_request = slot_of_page // per_request
    page_start = slot_of_page % per_request * page_size
    key_request = jnp.repeat(page_request, page_size)
    key_position = jnp.repeat(page_start, page_size) + jnp.tile(
        jnp.arange(page_size, dtype=jnp.int32), pages_here
    )
    request_ids = jnp.arange(req_count, dtype=jnp.int32)
    key_length = jnp.sum(
        (key_request[:, None] == request_ids[None, :]).astype(jnp.int32) * cache_lens[None, :],
        axis=1,
    )
    request_ends = jnp.cumsum(new_lens)
    tok_ids = jnp.arange(row_count, dtype=jnp.int32)
    tok_request = jnp.sum((tok_ids[:, None] >= request_ends[None, :]).astype(jnp.int32), axis=1)
    cached = (tok_request[:, None] == key_request[None, :]) & (key_position < key_length)[None, :]
    fresh_mask = tok_request[:, None] == tok_request[None, :]
    return jnp.concatenate([cached, fresh_mask], axis=1)


def dp_sum(part):
    n_dp = lax.axis_size("dp")
    me = lax.axis_index("dp")
    held = [part] + [
        lax.ppermute(part, "dp", [(i, (i + s) % n_dp) for i in range(n_dp)])
        for s in range(1, n_dp)
    ]
    total = None
    for j in range(n_dp):
        term = lax.select_n((me - j) % n_dp, *held).astype(jnp.float32)
        total = term if total is None else total + term
    return total


def one_hot_rows(slots, slot_count):
    hits = slots[None, :, :] == jnp.arange(slot_count, dtype=jnp.int32)[:, None, None]
    return jnp.any(hits, axis=2).astype(jnp.bfloat16)


def place_rows(pick, rows):
    return jnp.dot(pick, rows, preferred_element_type=jnp.float32).astype(jnp.bfloat16)


def expert_block(routed, w_gate, w_up, w_down):
    n_dp = lax.axis_size("dp")
    sources, local_experts, slots, width = routed.shape
    held = [(jnp.stack([w_gate, w_up]), w_down)]
    for s in range(1, n_dp):
        pairs = [(i, (i + s) % n_dp) for i in range(n_dp)]
        gate_up = lax.ppermute(held[0][0], "dp", pairs)
        down = lax.ppermute(held[0][1], "dp", pairs)
        held.append((gate_up, down))
    gate_up_all = jnp.concatenate([gate_up for gate_up, _ in held], axis=-1)
    block = held[0][1].shape[1]
    outs = []
    for e in range(local_experts):
        rows = routed[:, e].reshape(sources * slots, width)
        gate_proj = jnp.dot(rows, gate_up_all[0, e], preferred_element_type=jnp.float32)
        up_proj = jnp.dot(rows, gate_up_all[1, e], preferred_element_type=jnp.float32)
        active = (jax.nn.silu(gate_proj) * up_proj).astype(jnp.bfloat16)
        down_all = jnp.stack([down[e] for _, down in held])
        parts = jnp.einsum(
            "rnf,nfd->nrd",
            active.reshape(sources * slots, n_dp, block),
            down_all,
            preferred_element_type=jnp.float32,
        )
        parts = parts.astype(jnp.bfloat16).astype(jnp.float32)
        total = parts[0]
        for j in range(1, n_dp):
            total = total + parts[j]
        outs.append(total.reshape(sources, slots, width))
    return jnp.stack(outs, axis=1)


def local_body(
    tokens,
    attn_gain,
    w_query,
    w_key,
    w_value,
    w_out,
    cache,
    page_table,
    cache_len,
    new_len,
    kv_owner,
    moe_gain,
    w_gate,
    w_up,
    w_down,
    expert_ids,
    gate_weights,
):
    row_count, model_width = tokens.shape
    n_expert = lax.axis_size("expert")
    local_experts = w_gate.shape[0]
    experts_all = n_expert * local_experts
    top_count = expert_ids.shape[1]
    capacity = min(row_count, 2 * row_count * top_count // experts_all)
    kv_cap = max(2, 2 * row_count // n_expert)
    head_group = w_query.shape[1] // HD
    stacked = lax.all_gather(
        jnp.stack([w_query, w_key, w_value, w_out]), "expert", axis=1, tiled=True
    )
    full_query, full_key, full_value, full_out = (
        stacked[0],
        stacked[1],
        stacked[2],
        stacked[3],
    )
    resid_in = tokens.astype(jnp.float32)
    normed = norm_rows(resid_in, attn_gain)
    queries = jnp.dot(normed, full_query, preferred_element_type=jnp.float32).astype(jnp.bfloat16)
    new_keys = jnp.dot(normed, full_key, preferred_element_type=jnp.float32).astype(jnp.bfloat16)
    new_values = jnp.dot(normed, full_value, preferred_element_type=jnp.float32).astype(
        jnp.bfloat16
    )
    cache_count = cache.shape[0]
    split_cache = cache.reshape(cache_count, 2, head_group, HD)
    all_keys = jnp.concatenate(
        [split_cache[:, 0], new_keys.reshape(row_count, head_group, HD)], axis=0
    )
    all_values = jnp.concatenate(
        [split_cache[:, 1], new_values.reshape(row_count, head_group, HD)], axis=0
    )
    scores = jnp.einsum(
        "thc,rhc->htr",
        queries.reshape(row_count, head_group, HD),
        all_keys,
        preferred_element_type=jnp.float32,
    ) * HD ** (-0.5)
    valid_mask = key_masks(page_table[0], cache_len[0], new_len[0], row_count, PAGE)
    scores = jnp.where(valid_mask[None, :, :], scores, -1e30)
    highest = jnp.max(scores, axis=-1, keepdims=True)
    weights = jnp.exp(scores - highest)
    probs = (weights / jnp.sum(weights, axis=-1, keepdims=True)).astype(jnp.bfloat16)
    heads_out = (
        jnp.einsum("htr,rhc->thc", probs, all_values, preferred_element_type=jnp.float32)
        .astype(jnp.bfloat16)
        .reshape(row_count, head_group * HD)
    )
    attn_part = jnp.einsum("tc,dc->td", heads_out, full_out, preferred_element_type=jnp.float32)
    attn_out = dp_sum(attn_part.astype(jnp.bfloat16))
    residual = resid_in + attn_out
    moe_in = norm_rows(residual, moe_gain)
    kv_row = jnp.concatenate([new_keys, new_values], axis=1)
    kv_rank = route_rank(kv_owner, row_count, n_expert)[:, 0]
    kv_slot = kv_owner[:, 0] * kv_cap + kv_rank
    kv_pick = one_hot_rows(kv_slot[:, None], n_expert * kv_cap)
    kv_buffer = place_rows(kv_pick, kv_row).reshape(n_expert, kv_cap, kv_row.shape[1])
    n_dp = lax.axis_size("dp")
    me_dp = lax.axis_index("dp")
    quarter = capacity // n_dp
    slot_rank = route_rank(expert_ids, row_count, experts_all)
    in_quarter = slot_rank // quarter == me_dp
    q_slot = jnp.where(in_quarter, expert_ids * quarter + slot_rank % quarter, -1)
    tok_pick = one_hot_rows(q_slot, experts_all * quarter)
    tok_buffer = place_rows(tok_pick, moe_in).reshape(
        n_expert, local_experts, quarter, model_width
    )
    kv_width = kv_cap * kv_row.shape[1]
    extra = kv_width // quarter
    if local_experts == 1 and kv_width % quarter == 0 and extra % 128 == 0:
        send = jnp.concatenate(
            [tok_buffer, kv_buffer.reshape(n_expert, 1, quarter, extra)], axis=3
        )
        got = lax.all_to_all(send, "expert", split_axis=0, concat_axis=0, tiled=True)
        got_rows = got[:, :, :, :model_width]
        got_kv = got[:, :, :, model_width:].reshape(n_expert, kv_cap, kv_row.shape[1])
    else:
        got_rows = lax.all_to_all(tok_buffer, "expert", split_axis=0, concat_axis=0, tiled=True)
        got_kv = lax.all_to_all(kv_buffer, "expert", split_axis=0, concat_axis=0, tiled=True)
    contrib = expert_block(got_rows, w_gate, w_up, w_down)
    returned = lax.all_to_all(
        contrib.astype(jnp.bfloat16), "expert", split_axis=0, concat_axis=0, tiled=True
    ).reshape(experts_all * quarter, model_width)
    back_pick = (
        q_slot.reshape(-1)[:, None]
        == jnp.arange(experts_all * quarter, dtype=jnp.int32)[None, :]
    ).astype(jnp.bfloat16)
    picked = jnp.dot(back_pick, returned, preferred_element_type=jnp.float32).reshape(
        row_count, top_count, model_width
    )
    moe_part = jnp.sum(picked * gate_weights[:, :, None], axis=1)
    moe_total = dp_sum(moe_part.astype(jnp.bfloat16))
    out = (residual + moe_total).astype(jnp.bfloat16)
    new_rows = got_kv.reshape(n_expert * kv_cap, kv_row.shape[1])
    return (out, new_rows)


def solution(mesh):
    placed = (
        P("expert", None),
        P(),
        P("expert", "dp"),
        P("expert", "dp"),
        P("expert", "dp"),
        P("expert", "dp"),
        P("expert", "dp"),
        P("expert", None),
        P("expert", None),
        P("expert", None),
        P("expert", None),
        P(),
        P("expert", None, "dp"),
        P("expert", None, "dp"),
        P("expert", "dp", None),
        P("expert", None),
        P("expert", None),
    )
    return jax.shard_map(
        local_body,
        mesh=mesh,
        in_specs=placed,
        out_specs=(P("expert", None), P("expert", "dp")),
        check_vma=False,
    )
```

```python
import jax
import jax.numpy as jnp
from jax import lax
from jax.sharding import PartitionSpec as P


HD = 128
PAGE = 128


EPSILON = 1e-05


def norm_rows(row_data, gain_vec):
    mean_sq = jnp.mean(row_data * row_data, axis=-1, keepdims=True)
    return (row_data * lax.rsqrt(mean_sq + EPSILON) * gain_vec).astype(jnp.bfloat16)


def route_rank(route_ids, block_rows, id_range):
    row_total = route_ids.shape[0]
    labels = jnp.arange(id_range, dtype=jnp.int32)
    counts = jnp.sum((route_ids[:, :, None] == labels[None, None, :]).astype(jnp.int32), axis=1)
    counts = counts.reshape(row_total // block_rows, block_rows, id_range)
    before = (jnp.cumsum(counts, axis=1) - counts).reshape(row_total, id_range)
    return jnp.take_along_axis(before, route_ids, axis=1)


def key_masks(table_row, cache_lens, new_lens, row_count, page_size):
    req_count = cache_lens.shape[0]
    pages_here = table_row.shape[0]
    per_request = pages_here // req_count
    slot_ids = jnp.arange(pages_here, dtype=jnp.int32)
    matches = (table_row[:, None] == slot_ids[None, :]).astype(jnp.int32)
    slot_of_page = jnp.sum(matches * slot_ids[:, None], axis=0)
    page_request = slot_of_page // per_request
    page_start = slot_of_page % per_request * page_size
    key_request = jnp.repeat(page_request, page_size)
    key_position = jnp.repeat(page_start, page_size) + jnp.tile(
        jnp.arange(page_size, dtype=jnp.int32), pages_here
    )
    request_ids = jnp.arange(req_count, dtype=jnp.int32)
    key_length = jnp.sum(
        (key_request[:, None] == request_ids[None, :]).astype(jnp.int32) * cache_lens[None, :],
        axis=1,
    )
    request_ends = jnp.cumsum(new_lens)
    tok_ids = jnp.arange(row_count, dtype=jnp.int32)
    tok_request = jnp.sum((tok_ids[:, None] >= request_ends[None, :]).astype(jnp.int32), axis=1)
    cached = (tok_request[:, None] == key_request[None, :]) & (key_position < key_length)[None, :]
    fresh_mask = tok_request[:, None] == tok_request[None, :]
    return jnp.concatenate([cached, fresh_mask], axis=1)


def dp_sum(part):
    n_dp = lax.axis_size("dp")
    me = lax.axis_index("dp")
    held = [part] + [
        lax.ppermute(part, "dp", [(i, (i + s) % n_dp) for i in range(n_dp)])
        for s in range(1, n_dp)
    ]
    total = None
    for j in range(n_dp):
        term = lax.select_n((me - j) % n_dp, *held).astype(jnp.float32)
        total = term if total is None else total + term
    return total


def one_hot_rows(slots, slot_count):
    hits = slots[None, :, :] == jnp.arange(slot_count, dtype=jnp.int32)[:, None, None]
    return jnp.any(hits, axis=2).astype(jnp.bfloat16)


def place_rows(pick, rows):
    return jnp.dot(pick, rows, preferred_element_type=jnp.float32).astype(jnp.bfloat16)


def expert_block(routed, w_gate, w_up, w_down):
    n_dp = lax.axis_size("dp")
    sources, local_experts, slots, width = routed.shape
    held = [(jnp.stack([w_gate, w_up]), w_down)]
    for s in range(1, n_dp):
        pairs = [(i, (i + s) % n_dp) for i in range(n_dp)]
        gate_up = lax.ppermute(held[0][0], "dp", pairs)
        down = lax.ppermute(held[0][1], "dp", pairs)
        held.append((gate_up, down))
    gate_up_all = jnp.concatenate([gate_up for gate_up, _ in held], axis=-1)
    block = held[0][1].shape[1]
    outs = []
    for e in range(local_experts):
        rows = routed[:, e].reshape(sources * slots, width)
        gate_proj = jnp.dot(rows, gate_up_all[0, e], preferred_element_type=jnp.float32)
        up_proj = jnp.dot(rows, gate_up_all[1, e], preferred_element_type=jnp.float32)
        active = (jax.nn.silu(gate_proj) * up_proj).astype(jnp.bfloat16)
        down_all = jnp.stack([down[e] for _, down in held])
        parts = jnp.einsum(
            "rnf,nfd->nrd",
            active.reshape(sources * slots, n_dp, block),
            down_all,
            preferred_element_type=jnp.float32,
        )
        parts = parts.astype(jnp.bfloat16).astype(jnp.float32)
        total = parts[0]
        for j in range(1, n_dp):
            total = total + parts[j]
        outs.append(total.reshape(sources, slots, width))
    return jnp.stack(outs, axis=1)


def local_body(
    tokens,
    attn_gain,
    w_query,
    w_key,
    w_value,
    w_out,
    cache,
    page_table,
    cache_len,
    new_len,
    kv_owner,
    moe_gain,
    w_gate,
    w_up,
    w_down,
    expert_ids,
    gate_weights,
):
    row_count, model_width = tokens.shape
    n_expert = lax.axis_size("expert")
    local_experts = w_gate.shape[0]
    experts_all = n_expert * local_experts
    top_count = expert_ids.shape[1]
    capacity = min(row_count, 2 * row_count * top_count // experts_all)
    kv_cap = max(2, 2 * row_count // n_expert)
    head_group = w_query.shape[1] // HD
    stacked = lax.all_gather(
        jnp.stack([w_query, w_key, w_value, w_out]), "expert", axis=1, tiled=True
    )
    full_out = stacked[3]
    resid_in = tokens.astype(jnp.float32)
    normed = norm_rows(resid_in, attn_gain)
    projected = jnp.einsum(
        "td,wdc->wtc", normed, stacked[:3], preferred_element_type=jnp.float32
    ).astype(jnp.bfloat16)
    queries, new_keys, new_values = projected[0], projected[1], projected[2]
    cache_count = cache.shape[0]
    split_cache = cache.reshape(cache_count, 2, head_group, HD)
    all_keys = jnp.concatenate(
        [split_cache[:, 0], new_keys.reshape(row_count, head_group, HD)], axis=0
    )
    all_values = jnp.concatenate(
        [split_cache[:, 1], new_values.reshape(row_count, head_group, HD)], axis=0
    )
    scores = jnp.einsum(
        "thc,rhc->htr",
        queries.reshape(row_count, head_group, HD),
        all_keys,
        preferred_element_type=jnp.float32,
    ) * HD ** (-0.5)
    valid_mask = key_masks(page_table[0], cache_len[0], new_len[0], row_count, PAGE)
    scores = jnp.where(valid_mask[None, :, :], scores, -1e30)
    highest = jnp.max(scores, axis=-1, keepdims=True)
    weights = jnp.exp(scores - highest)
    probs = (weights / jnp.sum(weights, axis=-1, keepdims=True)).astype(jnp.bfloat16)
    heads_out = (
        jnp.einsum("htr,rhc->thc", probs, all_values, preferred_element_type=jnp.float32)
        .astype(jnp.bfloat16)
        .reshape(row_count, head_group * HD)
    )
    attn_part = jnp.einsum("tc,dc->td", heads_out, full_out, preferred_element_type=jnp.float32)
    attn_out = dp_sum(attn_part.astype(jnp.bfloat16))
    residual = resid_in + attn_out
    moe_in = norm_rows(residual, moe_gain)
    kv_row = jnp.concatenate([new_keys, new_values], axis=1)
    kv_rank = route_rank(kv_owner, row_count, n_expert)[:, 0]
    kv_slot = kv_owner[:, 0] * kv_cap + kv_rank
    kv_pick = one_hot_rows(kv_slot[:, None], n_expert * kv_cap)
    kv_buffer = place_rows(kv_pick, kv_row).reshape(n_expert, kv_cap, kv_row.shape[1])
    n_dp = lax.axis_size("dp")
    me_dp = lax.axis_index("dp")
    quarter = capacity // n_dp
    slot_rank = route_rank(expert_ids, row_count, experts_all)
    in_quarter = slot_rank // quarter == me_dp
    q_slot = jnp.where(in_quarter, expert_ids * quarter + slot_rank % quarter, -1)
    tok_pick = one_hot_rows(q_slot, experts_all * quarter)
    tok_buffer = place_rows(tok_pick, moe_in).reshape(
        n_expert, local_experts, quarter, model_width
    )
    kv_width = kv_cap * kv_row.shape[1]
    extra = kv_width // quarter
    if local_experts == 1 and kv_width % quarter == 0 and extra % 128 == 0:
        send = jnp.concatenate(
            [tok_buffer, kv_buffer.reshape(n_expert, 1, quarter, extra)], axis=3
        )
        got = lax.all_to_all(send, "expert", split_axis=0, concat_axis=0, tiled=True)
        got_rows = got[:, :, :, :model_width]
        got_kv = got[:, :, :, model_width:].reshape(n_expert, kv_cap, kv_row.shape[1])
    else:
        got_rows = lax.all_to_all(tok_buffer, "expert", split_axis=0, concat_axis=0, tiled=True)
        got_kv = lax.all_to_all(kv_buffer, "expert", split_axis=0, concat_axis=0, tiled=True)
    contrib = expert_block(got_rows, w_gate, w_up, w_down)
    returned = lax.all_to_all(
        contrib.astype(jnp.bfloat16), "expert", split_axis=0, concat_axis=0, tiled=True
    ).reshape(experts_all * quarter, model_width)
    back_pick = (
        q_slot.reshape(-1)[:, None]
        == jnp.arange(experts_all * quarter, dtype=jnp.int32)[None, :]
    ).astype(jnp.bfloat16)
    picked = jnp.dot(back_pick, returned, preferred_element_type=jnp.float32).reshape(
        row_count, top_count, model_width
    )
    moe_part = jnp.sum(picked * gate_weights[:, :, None], axis=1)
    moe_total = dp_sum(moe_part.astype(jnp.bfloat16))
    out = (residual + moe_total).astype(jnp.bfloat16)
    new_rows = got_kv.reshape(n_expert * kv_cap, kv_row.shape[1])
    return (out, new_rows)


def solution(mesh):
    placed = (
        P("expert", None),
        P(),
        P("expert", "dp"),
        P("expert", "dp"),
        P("expert", "dp"),
        P("expert", "dp"),
        P("expert", "dp"),
        P("expert", None),
        P("expert", None),
        P("expert", None),
        P("expert", None),
        P(),
        P("expert", None, "dp"),
        P("expert", None, "dp"),
        P("expert", "dp", None),
        P("expert", None),
        P("expert", None),
    )
    return jax.shard_map(
        local_body,
        mesh=mesh,
        in_specs=placed,
        out_specs=(P("expert", None), P("expert", "dp")),
        check_vma=False,
    )
```

```python
import jax
import jax.numpy as jnp
from jax import lax
from jax.sharding import PartitionSpec as P


HD = 128
PAGE = 128


EPSILON = 1e-05


def norm_rows(row_data, gain_vec):
    mean_sq = jnp.mean(row_data * row_data, axis=-1, keepdims=True)
    return (row_data * lax.rsqrt(mean_sq + EPSILON) * gain_vec).astype(jnp.bfloat16)


def route_rank(route_ids, block_rows, id_range):
    row_total = route_ids.shape[0]
    labels = jnp.arange(id_range, dtype=jnp.int32)
    counts = jnp.sum((route_ids[:, :, None] == labels[None, None, :]).astype(jnp.int32), axis=1)
    counts = counts.reshape(row_total // block_rows, block_rows, id_range)
    before = (jnp.cumsum(counts, axis=1) - counts).reshape(row_total, id_range)
    return jnp.take_along_axis(before, route_ids, axis=1)


def key_masks(table_row, cache_lens, new_lens, row_count, page_size):
    req_count = cache_lens.shape[0]
    pages_here = table_row.shape[0]
    per_request = pages_here // req_count
    slot_ids = jnp.arange(pages_here, dtype=jnp.int32)
    matches = (table_row[:, None] == slot_ids[None, :]).astype(jnp.int32)
    slot_of_page = jnp.sum(matches * slot_ids[:, None], axis=0)
    page_request = slot_of_page // per_request
    page_start = slot_of_page % per_request * page_size
    key_request = jnp.repeat(page_request, page_size)
    key_position = jnp.repeat(page_start, page_size) + jnp.tile(
        jnp.arange(page_size, dtype=jnp.int32), pages_here
    )
    request_ids = jnp.arange(req_count, dtype=jnp.int32)
    key_length = jnp.sum(
        (key_request[:, None] == request_ids[None, :]).astype(jnp.int32) * cache_lens[None, :],
        axis=1,
    )
    request_ends = jnp.cumsum(new_lens)
    tok_ids = jnp.arange(row_count, dtype=jnp.int32)
    tok_request = jnp.sum((tok_ids[:, None] >= request_ends[None, :]).astype(jnp.int32), axis=1)
    cached = (tok_request[:, None] == key_request[None, :]) & (key_position < key_length)[None, :]
    fresh_mask = tok_request[:, None] == tok_request[None, :]
    return jnp.concatenate([cached, fresh_mask], axis=1)


def dp_sum(part):
    n_dp = lax.axis_size("dp")
    me = lax.axis_index("dp")
    held = [part] + [
        lax.ppermute(part, "dp", [(i, (i + s) % n_dp) for i in range(n_dp)])
        for s in range(1, n_dp)
    ]
    total = None
    for j in range(n_dp):
        term = lax.select_n((me - j) % n_dp, *held).astype(jnp.float32)
        total = term if total is None else total + term
    return total


def one_hot_rows(slots, slot_count):
    hits = slots[None, :, :] == jnp.arange(slot_count, dtype=jnp.int32)[:, None, None]
    return jnp.any(hits, axis=2).astype(jnp.bfloat16)


def place_rows(pick, rows):
    return jnp.dot(pick, rows, preferred_element_type=jnp.float32).astype(jnp.bfloat16)


def expert_block(routed, w_gate, w_up, w_down):
    n_dp = lax.axis_size("dp")
    sources, local_experts, slots, width = routed.shape
    held = [(jnp.stack([w_gate, w_up]), w_down)]
    for s in range(1, n_dp):
        pairs = [(i, (i + s) % n_dp) for i in range(n_dp)]
        gate_up = lax.ppermute(held[0][0], "dp", pairs)
        down = lax.ppermute(held[0][1], "dp", pairs)
        held.append((gate_up, down))
    gate_up_all = jnp.concatenate([gate_up for gate_up, _ in held], axis=-1)
    block = held[0][1].shape[1]
    outs = []
    for e in range(local_experts):
        rows = routed[:, e].reshape(sources * slots, width)
        gate_proj = jnp.dot(rows, gate_up_all[0, e], preferred_element_type=jnp.float32)
        up_proj = jnp.dot(rows, gate_up_all[1, e], preferred_element_type=jnp.float32)
        active = (jax.nn.silu(gate_proj) * up_proj).astype(jnp.bfloat16)
        down_all = jnp.stack([down[e] for _, down in held])
        parts = jnp.einsum(
            "rnf,nfd->nrd",
            active.reshape(sources * slots, n_dp, block),
            down_all,
            preferred_element_type=jnp.float32,
        )
        parts = parts.astype(jnp.bfloat16).astype(jnp.float32)
        total = parts[0]
        for j in range(1, n_dp):
            total = total + parts[j]
        outs.append(total.reshape(sources, slots, width))
    return jnp.stack(outs, axis=1)


def local_body(
    tokens,
    attn_gain,
    w_query,
    w_key,
    w_value,
    w_out,
    cache,
    page_table,
    cache_len,
    new_len,
    kv_owner,
    moe_gain,
    w_gate,
    w_up,
    w_down,
    expert_ids,
    gate_weights,
):
    row_count, model_width = tokens.shape
    n_expert = lax.axis_size("expert")
    local_experts = w_gate.shape[0]
    experts_all = n_expert * local_experts
    top_count = expert_ids.shape[1]
    capacity = min(row_count, 2 * row_count * top_count // experts_all)
    kv_cap = max(2, 2 * row_count // n_expert)
    head_group = w_query.shape[1] // HD
    stacked = lax.all_gather(
        jnp.stack([w_query, w_key, w_value, w_out]), "expert", axis=1, tiled=True
    )
    full_out = stacked[3]
    resid_in = tokens.astype(jnp.float32)
    normed = norm_rows(resid_in, attn_gain)
    projected = jnp.einsum(
        "td,wdc->wtc", normed, stacked[:3], preferred_element_type=jnp.float32
    ).astype(jnp.bfloat16)
    queries, new_keys, new_values = projected[0], projected[1], projected[2]
    cache_count = cache.shape[0]
    split_cache = cache.reshape(cache_count, 2, head_group, HD)
    all_keys = jnp.concatenate(
        [split_cache[:, 0], new_keys.reshape(row_count, head_group, HD)], axis=0
    )
    all_values = jnp.concatenate(
        [split_cache[:, 1], new_values.reshape(row_count, head_group, HD)], axis=0
    )
    scores = jnp.einsum(
        "thc,rhc->htr",
        queries.reshape(row_count, head_group, HD),
        all_keys,
        preferred_element_type=jnp.float32,
    ) * HD ** (-0.5)
    valid_mask = key_masks(page_table[0], cache_len[0], new_len[0], row_count, PAGE)
    scores = jnp.where(valid_mask[None, :, :], scores, -1e30)
    highest = jnp.max(scores, axis=-1, keepdims=True)
    weights = jnp.exp(scores - highest)
    probs = (weights / jnp.sum(weights, axis=-1, keepdims=True)).astype(jnp.bfloat16)
    heads_out = (
        jnp.einsum("htr,rhc->thc", probs, all_values, preferred_element_type=jnp.float32)
        .astype(jnp.bfloat16)
        .reshape(row_count, head_group * HD)
    )
    attn_part = jnp.einsum("tc,dc->td", heads_out, full_out, preferred_element_type=jnp.float32)
    attn_out = dp_sum(attn_part.astype(jnp.bfloat16))
    residual = resid_in + attn_out
    moe_in = norm_rows(residual, moe_gain)
    kv_row = jnp.concatenate([new_keys, new_values], axis=1)
    kv_rank = route_rank(kv_owner, row_count, n_expert)[:, 0]
    kv_slot = kv_owner[:, 0] * kv_cap + kv_rank
    kv_pick = one_hot_rows(kv_slot[:, None], n_expert * kv_cap)
    kv_buffer = place_rows(kv_pick, kv_row).reshape(n_expert, kv_cap, kv_row.shape[1])
    n_dp = lax.axis_size("dp")
    me_dp = lax.axis_index("dp")
    quarter = capacity // n_dp
    slot_rank = route_rank(expert_ids, row_count, experts_all)
    in_quarter = slot_rank // quarter == me_dp
    q_slot = jnp.where(in_quarter, expert_ids * quarter + slot_rank % quarter, -1)
    tok_pick = one_hot_rows(q_slot, experts_all * quarter)
    tok_buffer = place_rows(tok_pick, moe_in).reshape(
        n_expert, local_experts, quarter, model_width
    )
    kv_width = kv_cap * kv_row.shape[1]
    extra = kv_width // quarter
    if local_experts == 1 and kv_width % quarter == 0 and extra % 128 == 0:
        send = jnp.concatenate(
            [tok_buffer, kv_buffer.reshape(n_expert, 1, quarter, extra)], axis=3
        )
        got = lax.all_to_all(send, "expert", split_axis=0, concat_axis=0, tiled=True)
        got_rows = got[:, :, :, :model_width]
        got_kv = got[:, :, :, model_width:].reshape(n_expert, kv_cap, kv_row.shape[1])
    else:
        got_rows = lax.all_to_all(tok_buffer, "expert", split_axis=0, concat_axis=0, tiled=True)
        got_kv = lax.all_to_all(kv_buffer, "expert", split_axis=0, concat_axis=0, tiled=True)
    contrib = expert_block(got_rows, w_gate, w_up, w_down)
    returned = lax.all_to_all(
        contrib.astype(jnp.bfloat16), "expert", split_axis=0, concat_axis=0, tiled=True
    ).reshape(experts_all * quarter, model_width)
    hits = q_slot[:, :, None] == jnp.arange(experts_all * quarter, dtype=jnp.int32)[None, None, :]
    weighting = jnp.sum(jnp.where(hits, gate_weights[:, :, None], 0.0), axis=1)
    moe_part = jnp.dot(
        weighting,
        returned.astype(jnp.float32),
        precision=lax.Precision.HIGHEST,
        preferred_element_type=jnp.float32,
    )
    moe_total = dp_sum(moe_part.astype(jnp.bfloat16))
    out = (residual + moe_total).astype(jnp.bfloat16)
    new_rows = got_kv.reshape(n_expert * kv_cap, kv_row.shape[1])
    return (out, new_rows)


def solution(mesh):
    placed = (
        P("expert", None),
        P(),
        P("expert", "dp"),
        P("expert", "dp"),
        P("expert", "dp"),
        P("expert", "dp"),
        P("expert", "dp"),
        P("expert", None),
        P("expert", None),
        P("expert", None),
        P("expert", None),
        P(),
        P("expert", None, "dp"),
        P("expert", None, "dp"),
        P("expert", "dp", None),
        P("expert", None),
        P("expert", None),
    )
    return jax.shard_map(
        local_body,
        mesh=mesh,
        in_specs=placed,
        out_specs=(P("expert", None), P("expert", "dp")),
        check_vma=False,
    )
```
